512 devices in a mesh: lon: 32 (over z, x_hi), lat: 16 (over x_lo, y, core).
Axes of the slice: x: 4 (x_hi: 2, x_lo: 2; x = x_hi * 2 + x_lo), y: 4, z: 16, core: 2. Of those that a mesh axis runs over, the one named last changes fastest.
Arguments:
- elevation: float32 [12, 1536, 4096], P(None, 'lat', 'lon'), may hold values from -6 to 6
- equilibrium: float32 [12, 1536, 4096], P(None, 'lat', 'lon'), may hold values from -4 to 4
- transport_u: float32 [12, 1536, 4096], P(None, 'lat', 'lon'), may hold values from -4 to 4
- transport_v: float32 [12, 1536, 4096], P(None, 'lat', 'lon'), may hold values from -4 to 4
- ocean_depth: float32 [1536, 4096], P('lat', 'lon'), may hold values from 0.3 to 3
- bottom_drag: float32 [1536, 4096], P('lat', 'lon'), may hold values from 0.2 to 2
- wet_mask: int32 [1536, 4096], P('lat', 'lon'), may hold values 0 or 1
- lon_green: float32 [4096, 128], P('lon'), may hold values from -0.5 to 0.5
- lat_green: float32 [1536, 49152], P('lat', 'lon'), may hold values from -0.0546875 to 0.0546875
Outputs:
- elevation_next: float32 [12, 1536, 4096], P(None, 'lat', 'lon')
- transport_u_next: float32 [12, 1536, 4096], P(None, 'lat', 'lon')
- transport_v_next: float32 [12, 1536, 4096], P(None, 'lat', 'lon')
The draws below stay inside these ranges and needn't reach their ends.
All inputs are finite; a program needn't handle non-finite values. No bound on the sum of `wet_mask` on one device may be relied on, other than what follows from the above.
Results may differ from the reference program's by a relative error of at most 0.0001.
Values sent between devices are 32-bit elements; how exact they have to be, the bound alone decides.
No kernel may reach another device: no remote copies, remote signals or barrier semaphores. Data moves between devices by JAX's collectives and lax.ppermute only.
A program may use at most 64 MiB of HBM per device.

```python
import math
import jax
import jax.numpy as jnp
from jax import lax

COLUMNS = 12
TX = 128
NLAT = 1536
NLON = 4096
N_LON = 32


def touch_ends(result, own_key, low, largest):
    place = [jax.random.randint(jax.random.fold_in(own_key, axis), (), 0, length) for axis, length in enumerate(result.shape)]
    longest = result.shape.index(max(result.shape))
    beside = place[:longest] + [(place[longest] + 1) % result.shape[longest]] + place[longest + 1:]
    return result.at[tuple(place)].set(low).at[tuple(beside)].set(largest)


def shard_levels(stream_key, shape, split, least, high):
    level = 1.0
    for position, shards_of in split:
        draws = jax.random.uniform(jax.random.fold_in(jax.random.fold_in(stream_key, 6), position), (shards_of,), jnp.float32, least / len(split), high / len(split))
        level = level * jnp.repeat(jnp.exp(draws), shape[position] // shards_of).reshape((-1,) + (1,) * (len(shape) - 1 - position))
    return level


def bell_draw(own_key, shape, scale, reach, cuts=(), kind=jnp.bfloat16):
    drawn = jax.random.normal(own_key, shape, jnp.float32) * scale
    if len(cuts) > 0:
        drawn = shard_levels(own_key, shape, cuts, -0.22, 0.18) * drawn
    return jnp.clip(drawn, min=-reach, max=reach).astype(kind)


def setup_inputs(seed: int = 0) -> dict:
    arg_keys = jax.random.split(jax.random.key(seed), 10)
    return {
        "elevation": bell_draw(arg_keys[0], (COLUMNS, NLAT, NLON), 1.0, 6.0, ((1, 16), (2, 32)), jnp.float32),
        "equilibrium": bell_draw(arg_keys[1], (COLUMNS, NLAT, NLON), 0.5, 4.0, ((1, 16), (2, 32)), jnp.float32),
        "transport_u": bell_draw(arg_keys[2], (COLUMNS, NLAT, NLON), 0.5, 4.0, ((1, 16), (2, 32)), jnp.float32),
        "transport_v": bell_draw(arg_keys[3], (COLUMNS, NLAT, NLON), 0.5, 4.0, ((1, 16), (2, 32)), jnp.float32),
        "ocean_depth": jnp.clip(jnp.exp(math.log(3.0) - 2.3025851 * jax.random.uniform(arg_keys[4], (NLAT, NLON), jnp.float32) ** shard_levels(arg_keys[4], (NLAT, NLON), ((0, 16), (1, 32)), -0.2, 0.2)), 0.3, 3.0),
        "bottom_drag": jnp.clip(jnp.exp(math.log(2.0) - 2.3025851 * jax.random.uniform(arg_keys[5], (NLAT, NLON), jnp.float32) ** shard_levels(arg_keys[5], (NLAT, NLON), ((0, 16), (1, 32)), -0.2, 0.2)), 0.2, 2.0),
        "wet_mask": touch_ends((jax.random.randint(arg_keys[6], (NLAT, NLON), 0, 10) < 7).astype(jnp.int32), jax.random.fold_in(arg_keys[6], 1), 0, 1),
        "lon_green": bell_draw(arg_keys[7], (NLON, TX), TX ** -0.5, 0.5, ((0, 32),), jnp.float32),
        "lat_green": bell_draw(arg_keys[8], (NLAT, NLAT * N_LON), (9 * NLAT) ** -0.5, 0.0546875, ((0, 16), (1, 32)), jnp.float32),
    }


FREQS = [1.9323, 2.0, 1.8960, 2.0055, 1.0027, 0.9295]
VISCOSITY = 0.5


def row_terms(rows, nlat):
    angle = (-80.0 + 160.0 * (rows.astype(jnp.float32) + 0.5) / nlat) * (math.pi / 180.0)
    return (1.0 / jnp.cos(angle))[:, None], (2.0 * jnp.sin(angle))[:, None]


def extend_full(field, width):
    field = jnp.concatenate([field[:, :, -width:], field, field[:, :, :width]], axis=2)
    return jnp.pad(field, ((0, 0), (width, width), (0, 0)))


def slopes(potential_ext, stretch):
    east_slope = (potential_ext[:, 1:-1, 2:] - potential_ext[:, 1:-1, :-2]) * 0.5 * stretch
    north_slope = (potential_ext[:, 2:, 1:-1] - potential_ext[:, :-2, 1:-1]) * 0.5
    return east_slope, north_slope


def solve_cells(push_u, push_v, depth_field, drag_field, wet_frac, coriolis):
    damping = drag_field + 4.0 * VISCOSITY
    frequency = jnp.array(FREQS, jnp.float32)[:, None, None]
    det_real = damping * damping - frequency * frequency + coriolis * coriolis
    det_imag = 2.0 * damping * frequency
    magnitude = det_real * det_real + det_imag * det_imag

    def combine(first, second, factor):
        top_real = damping * first[:6] - frequency * first[6:] + factor * coriolis * second[:6]
        top_imag = damping * first[6:] + frequency * first[:6] + factor * coriolis * second[6:]
        out_real = (top_real * det_real + top_imag * det_imag) / magnitude
        out_imag = (top_imag * det_real - top_real * det_imag) / magnitude
        return wet_frac * jnp.concatenate([out_real, out_imag], axis=0)

    return jnp.concatenate([combine(push_u, push_v, 1.0), combine(push_v, push_u, -1.0)], axis=0)


def relax(flow_ext, east_slope, north_slope, depth_field, drag_field, wet_frac, coriolis):
    beside_all = flow_ext[:, :-2, 1:-1] + flow_ext[:, 2:, 1:-1] + flow_ext[:, 1:-1, :-2] + flow_ext[:, 1:-1, 2:]
    push_u = -depth_field * east_slope + VISCOSITY * beside_all[:12]
    push_v = -depth_field * north_slope + VISCOSITY * beside_all[12:]
    return solve_cells(push_u, push_v, depth_field, drag_field, wet_frac, coriolis)


def surface(east_ext, north_ext, stretch, wet_frac):
    spread = (east_ext[:, :, 2:] - east_ext[:, :, :-2]) * 0.5 * stretch + (north_ext[:, 2:, :] - north_ext[:, :-2, :]) * 0.5
    frequency = jnp.array(FREQS, jnp.float32)[:, None, None]
    return wet_frac * jnp.concatenate([-spread[6:] / frequency, spread[:6] / frequency], axis=0)


def reference(elevation, equilibrium, transport_u, transport_v, ocean_depth, bottom_drag, wet_mask, lon_green, lat_green):
    wet_frac = wet_mask.astype(jnp.float32)
    source = wet_frac * elevation
    blocks = source.reshape(12, NLAT, N_LON, TX)
    lon_blocks = lon_green.reshape(N_LON, TX, TX)
    mixed = jnp.einsum('krbj,bcj->krbc', blocks, lon_blocks, precision=lax.Precision.HIGHEST)
    lat_blocks = lat_green.reshape(NLAT, N_LON, NLAT)
    sal = jnp.einsum('rbs,ksbc->krbc', lat_blocks, mixed, precision=lax.Precision.HIGHEST).reshape(12, NLAT, NLON)
    potential = elevation - equilibrium - sal
    stretch, coriolis = row_terms(jnp.arange(NLAT), NLAT)
    east_slope, north_slope = slopes(extend_full(potential, 1), stretch)
    flows = jnp.concatenate([transport_u, transport_v], axis=0)
    for sweep_index in range(2):
        flows = relax(extend_full(flows, 1), east_slope, north_slope, ocean_depth, bottom_drag, wet_frac, coriolis)
    widened = extend_full(flows, 1)
    elevation_next = surface(widened[:12, 1:-1, :], widened[12:, :, 1:-1], stretch, wet_frac)
    return elevation_next, flows[:12], flows[12:]
```

```python
import math

import jax
import jax.numpy as jnp
from jax import lax
from jax.sharding import Mesh
from jax.sharding import PartitionSpec as P

FREQS = [1.9323, 2.0, 1.896, 2.0055, 1.0027, 0.9295]
VISCOSITY = 0.5
HALO = 3
LAT = ("chip", "core")


def lat_index():
    return lax.axis_index("chip") * lax.axis_size("core") + lax.axis_index("core")


def lat_size():
    return lax.axis_size("chip") * lax.axis_size("core")


def widen_lon(array, width, dim):
    size, length = lax.axis_size("lon"), array.shape[dim]
    up = [(i, (i + 1) % size) for i in range(size)]
    down = [(j, i) for i, j in up]
    last = lax.slice_in_dim(array, length - width, length, axis=dim)
    initial = lax.slice_in_dim(array, 0, width, axis=dim)
    before = lax.ppermute(last, "lon", up)
    after = lax.ppermute(initial, "lon", down)
    return jnp.concatenate([before, array, after], axis=dim)


def widen_lat(array, width, dim):
    size, length = lat_size(), array.shape[dim]
    up = [(i, i + 1) for i in range(size - 1)]
    down = [(j, i) for i, j in up]
    last = lax.slice_in_dim(array, length - width, length, axis=dim)
    initial = lax.slice_in_dim(array, 0, width, axis=dim)
    before = lax.ppermute(last, LAT, up)
    after = lax.ppermute(initial, LAT, down)
    return jnp.concatenate([before, array, after], axis=dim)


def row_terms(rows, nlat):
    angle = (-80.0 + 160.0 * (rows.astype(jnp.float32) + 0.5) / nlat) * (math.pi / 180.0)
    return ((1.0 / jnp.cos(angle))[:, None], (2.0 * jnp.sin(angle))[:, None])


def slopes(potential_ext, stretch):
    east_slope = (potential_ext[:, 1:-1, 2:] - potential_ext[:, 1:-1, :-2]) * 0.5 * stretch
    north_slope = (potential_ext[:, 2:, 1:-1] - potential_ext[:, :-2, 1:-1]) * 0.5
    return (east_slope, north_slope)


def solve_cells(push_u, push_v, drag_field, wet_frac, coriolis):
    damping = drag_field + 4.0 * VISCOSITY
    frequency = jnp.array(FREQS, jnp.float32)[:, None, None]
    det_real = damping * damping - frequency * frequency + coriolis * coriolis
    det_imag = 2.0 * damping * frequency
    magnitude = det_real * det_real + det_imag * det_imag

    def combine(first, second, factor):
        top_real = damping * first[:6] - frequency * first[6:] + factor * coriolis * second[:6]
        top_imag = damping * first[6:] + frequency * first[:6] + factor * coriolis * second[6:]
        out_real = (top_real * det_real + top_imag * det_imag) / magnitude
        out_imag = (top_imag * det_real - top_real * det_imag) / magnitude
        return wet_frac * jnp.concatenate([out_real, out_imag], axis=0)

    return jnp.concatenate([combine(push_u, push_v, 1.0), combine(push_v, push_u, -1.0)], axis=0)


def inner(field, trim):
    return field[..., trim : field.shape[-2] - trim, trim : field.shape[-1] - trim]


def relax(flow_ext, east_slope, north_slope, depth_field, drag_field, wet_frac, coriolis):
    beside_all = (
        flow_ext[:, :-2, 1:-1]
        + flow_ext[:, 2:, 1:-1]
        + flow_ext[:, 1:-1, :-2]
        + flow_ext[:, 1:-1, 2:]
    )
    push_u = -depth_field * east_slope + VISCOSITY * beside_all[:12]
    push_v = -depth_field * north_slope + VISCOSITY * beside_all[12:]
    return solve_cells(push_u, push_v, drag_field, wet_frac, coriolis)


def surface(east_ext, north_ext, stretch, wet_frac):
    spread = (east_ext[:, :, 2:] - east_ext[:, :, :-2]) * 0.5 * stretch + (
        north_ext[:, 2:, :] - north_ext[:, :-2, :]
    ) * 0.5
    frequency = jnp.array(FREQS, jnp.float32)[:, None, None]
    return wet_frac * jnp.concatenate([-spread[6:] / frequency, spread[:6] / frequency], axis=0)


def per_device(
    elevation,
    equilibrium,
    transport_u,
    transport_v,
    ocean_depth,
    bottom_drag,
    wet_mask,
    lon_green,
    lat_green,
):
    rows_here = elevation.shape[1]
    total_rows = rows_here * lat_size()
    wet_frac = wet_mask.astype(jnp.float32)
    source = wet_frac * elevation
    mixed = jnp.einsum("krj,cj->krc", source, lon_green, precision=lax.Precision.HIGHEST)
    gathered = lax.all_gather(mixed, LAT, axis=1, tiled=True)

    fields = jnp.stack([ocean_depth, bottom_drag, wet_frac], axis=0)
    stack = jnp.concatenate([elevation - equilibrium, transport_u, transport_v, fields], axis=0)
    stack = widen_lat(widen_lon(stack, HALO, 2), HALO, 1)
    green_ext = widen_lat(lat_green, HALO, 0)

    sal = jnp.einsum("rs,ksc->krc", green_ext, gathered, precision=lax.Precision.HIGHEST)
    sal = widen_lon(sal, HALO, 2)
    potential = stack[:12] - sal
    flows = stack[12:36]
    depth_ext, drag_ext, wet_ext = stack[36], stack[37], stack[38]

    first_row = lat_index() * rows_here - HALO
    stretch, coriolis = row_terms(first_row + jnp.arange(rows_here + 2 * HALO), total_rows)
    east_slope, north_slope = slopes(potential, stretch[1:-1])
    flows = relax(
        flows,
        east_slope,
        north_slope,
        inner(depth_ext, 1),
        inner(drag_ext, 1),
        inner(wet_ext, 1),
        coriolis[1:-1],
    )
    flows = relax(
        flows,
        inner(east_slope, 1),
        inner(north_slope, 1),
        inner(depth_ext, 2),
        inner(drag_ext, 2),
        inner(wet_ext, 2),
        coriolis[2:-2],
    )
    east_ext = flows[:12, 1:-1, :]
    north_ext = flows[12:, :, 1:-1]
    elevation_next = surface(east_ext, north_ext, stretch[HALO:-HALO], wet_frac)
    flows = inner(flows, 1)
    return (elevation_next, flows[:12], flows[12:])


def solution(mesh):
    lat_devices = mesh.shape["lat"]
    cores = 2 if lat_devices % 2 == 0 else 1
    devices = mesh.devices.reshape(mesh.shape["lon"], lat_devices // cores, cores)
    split = Mesh(devices, ("lon", "chip", "core"))
    grid = P(None, LAT, "lon")
    plane = P(LAT, "lon")
    placed = (grid, grid, grid, grid, plane, plane, plane, P("lon", None), plane)
    return jax.shard_map(
        per_device,
        mesh=split,
        in_specs=placed,
        out_specs=(grid, grid, grid),
        check_vma=False,
    )
```

```python
import math

import jax
import jax.numpy as jnp
from jax import lax
from jax.sharding import Mesh
from jax.sharding import PartitionSpec as P

FREQS = [1.9323, 2.0, 1.896, 2.0055, 1.0027, 0.9295]
VISCOSITY = 0.5
HALO = 3
LAT = ("half", "row", "core")
ROW = ("row", "core")


def lat_index():
    return (
        lax.axis_index("half") * lax.axis_size("row") + lax.axis_index("row")
    ) * lax.axis_size("core") + lax.axis_index("core")


def lat_size():
    return lax.axis_size("half") * lax.axis_size("row") * lax.axis_size("core")


def widen_lon(array, width, dim):
    size, length = lax.axis_size("lon"), array.shape[dim]
    up = [(i, (i + 1) % size) for i in range(size)]
    down = [(j, i) for i, j in up]
    last = lax.slice_in_dim(array, length - width, length, axis=dim)
    initial = lax.slice_in_dim(array, 0, width, axis=dim)
    before = lax.ppermute(last, "lon", up)
    after = lax.ppermute(initial, "lon", down)
    return jnp.concatenate([before, array, after], axis=dim)


def widen_lat(array, width, dim):
    size, length = lat_size(), array.shape[dim]
    up = [(i, i + 1) for i in range(size - 1)]
    down = [(j, i) for i, j in up]
    last = lax.slice_in_dim(array, length - width, length, axis=dim)
    initial = lax.slice_in_dim(array, 0, width, axis=dim)
    before = lax.ppermute(last, LAT, up)
    after = lax.ppermute(initial, LAT, down)
    return jnp.concatenate([before, array, after], axis=dim)


def row_terms(rows, nlat):
    angle = (-80.0 + 160.0 * (rows.astype(jnp.float32) + 0.5) / nlat) * (math.pi / 180.0)
    return ((1.0 / jnp.cos(angle))[:, None], (2.0 * jnp.sin(angle))[:, None])


def slopes(potential_ext, stretch):
    east_slope = (potential_ext[:, 1:-1, 2:] - potential_ext[:, 1:-1, :-2]) * 0.5 * stretch
    north_slope = (potential_ext[:, 2:, 1:-1] - potential_ext[:, :-2, 1:-1]) * 0.5
    return (east_slope, north_slope)


def solve_cells(push_u, push_v, drag_field, wet_frac, coriolis):
    damping = drag_field + 4.0 * VISCOSITY
    frequency = jnp.array(FREQS, jnp.float32)[:, None, None]
    det_real = damping * damping - frequency * frequency + coriolis * coriolis
    det_imag = 2.0 * damping * frequency
    magnitude = det_real * det_real + det_imag * det_imag

    def combine(first, second, factor):
        top_real = damping * first[:6] - frequency * first[6:] + factor * coriolis * second[:6]
        top_imag = damping * first[6:] + frequency * first[:6] + factor * coriolis * second[6:]
        out_real = (top_real * det_real + top_imag * det_imag) / magnitude
        out_imag = (top_imag * det_real - top_real * det_imag) / magnitude
        return wet_frac * jnp.concatenate([out_real, out_imag], axis=0)

    return jnp.concatenate([combine(push_u, push_v, 1.0), combine(push_v, push_u, -1.0)], axis=0)


def inner(field, trim):
    return field[..., trim : field.shape[-2] - trim, trim : field.shape[-1] - trim]


def relax(flow_ext, east_slope, north_slope, depth_field, drag_field, wet_frac, coriolis):
    beside_all = (
        flow_ext[:, :-2, 1:-1]
        + flow_ext[:, 2:, 1:-1]
        + flow_ext[:, 1:-1, :-2]
        + flow_ext[:, 1:-1, 2:]
    )
    push_u = -depth_field * east_slope + VISCOSITY * beside_all[:12]
    push_v = -depth_field * north_slope + VISCOSITY * beside_all[12:]
    return solve_cells(push_u, push_v, drag_field, wet_frac, coriolis)


def surface(east_ext, north_ext, stretch, wet_frac):
    spread = (east_ext[:, :, 2:] - east_ext[:, :, :-2]) * 0.5 * stretch + (
        north_ext[:, 2:, :] - north_ext[:, :-2, :]
    ) * 0.5
    frequency = jnp.array(FREQS, jnp.float32)[:, None, None]
    return wet_frac * jnp.concatenate([-spread[6:] / frequency, spread[:6] / frequency], axis=0)


def per_device(
    elevation,
    equilibrium,
    transport_u,
    transport_v,
    ocean_depth,
    bottom_drag,
    wet_mask,
    lon_green,
    lat_green,
):
    rows_here = elevation.shape[1]
    total_rows = rows_here * lat_size()
    wet_frac = wet_mask.astype(jnp.float32)
    source = wet_frac * elevation
    mixed = jnp.einsum("krj,cj->krc", source, lon_green, precision=lax.Precision.HIGHEST)
    gathered = lax.all_gather(mixed, ROW, axis=1, tiled=True)

    fields = jnp.stack([ocean_depth, bottom_drag, wet_frac], axis=0)
    stack = jnp.concatenate([elevation - equilibrium, transport_u, transport_v, fields], axis=0)
    stack = widen_lat(widen_lon(stack, HALO, 2), HALO, 1)
    green_ext = widen_lat(lat_green, HALO, 0)

    halves = lax.axis_size("half")
    half = lax.axis_index("half")
    green_split = green_ext.reshape(green_ext.shape[0], halves, -1)
    swap = [(i, (i + 1) % halves) for i in range(halves)]
    green_away = lax.ppermute(
        lax.dynamic_index_in_dim(green_split, (half + 1) % halves, axis=1, keepdims=False), "half", swap
    )
    green_home = lax.dynamic_index_in_dim(green_split, half, axis=1, keepdims=False)
    for_partner = jnp.einsum("rs,ksc->krc", green_away, gathered, precision=lax.Precision.HIGHEST)
    back = [(j, i) for i, j in swap]
    from_partner = lax.ppermute(for_partner, "half", back)
    sal = jnp.einsum("rs,ksc->krc", green_home, gathered, precision=lax.Precision.HIGHEST)
    sal = sal + from_partner
    sal = widen_lon(sal, HALO, 2)
    potential = stack[:12] - sal
    flows = stack[12:36]
    depth_ext, drag_ext, wet_ext = stack[36], stack[37], stack[38]

    first_row = lat_index() * rows_here - HALO
    stretch, coriolis = row_terms(first_row + jnp.arange(rows_here + 2 * HALO), total_rows)
    east_slope, north_slope = slopes(potential, stretch[1:-1])
    flows = relax(
        flows,
        east_slope,
        north_slope,
        inner(depth_ext, 1),
        inner(drag_ext, 1),
        inner(wet_ext, 1),
        coriolis[1:-1],
    )
    flows = relax(
        flows,
        inner(east_slope, 1),
        inner(north_slope, 1),
        inner(depth_ext, 2),
        inner(drag_ext, 2),
        inner(wet_ext, 2),
        coriolis[2:-2],
    )
    east_ext = flows[:12, 1:-1, :]
    north_ext = flows[12:, :, 1:-1]
    elevation_next = surface(east_ext, north_ext, stretch[HALO:-HALO], wet_frac)
    flows = inner(flows, 1)
    return (elevation_next, flows[:12], flows[12:])


def solution(mesh):
    lat_devices = mesh.shape["lat"]
    devices = mesh.devices.reshape(mesh.shape["lon"], 2, lat_devices // 4, 2)
    split = Mesh(devices, ("lon", "half", "row", "core"))
    grid = P(None, LAT, "lon")
    plane = P(LAT, "lon")
    placed = (grid, grid, grid, grid, plane, plane, plane, P("lon", None), plane)
    return jax.shard_map(
        per_device,
        mesh=split,
        in_specs=placed,
        out_specs=(grid, grid, grid),
        check_vma=False,
    )
```

```python
import math

import jax
import jax.numpy as jnp
from jax import lax
from jax.sharding import Mesh
from jax.sharding import PartitionSpec as P

FREQS = [1.9323, 2.0, 1.896, 2.0055, 1.0027, 0.9295]
VISCOSITY = 0.5
HALO = 3
LAT = ("chip", "core")


def lat_index():
    return lax.axis_index("chip") * lax.axis_size("core") + lax.axis_index("core")


def lat_size():
    return lax.axis_size("chip") * lax.axis_size("core")


def widen_lon(array, width, dim):
    size, length = lax.axis_size("lon"), array.shape[dim]
    up = [(i, (i + 1) % size) for i in range(size)]
    down = [(j, i) for i, j in up]
    last = lax.slice_in_dim(array, length - width, length, axis=dim)
    initial = lax.slice_in_dim(array, 0, width, axis=dim)
    before = lax.ppermute(last, "lon", up)
    after = lax.ppermute(initial, "lon", down)
    return jnp.concatenate([before, array, after], axis=dim)


def widen_lat(array, width, dim):
    size, length = lat_size(), array.shape[dim]
    up = [(i, i + 1) for i in range(size - 1)]
    down = [(j, i) for i, j in up]
    last = lax.slice_in_dim(array, length - width, length, axis=dim)
    initial = lax.slice_in_dim(array, 0, width, axis=dim)
    before = lax.ppermute(last, LAT, up)
    after = lax.ppermute(initial, LAT, down)
    return jnp.concatenate([before, array, after], axis=dim)


def row_terms(rows, nlat):
    angle = (-80.0 + 160.0 * (rows.astype(jnp.float32) + 0.5) / nlat) * (math.pi / 180.0)
    return ((1.0 / jnp.cos(angle))[:, None], (2.0 * jnp.sin(angle))[:, None])


def slopes(potential_ext, stretch):
    east_slope = (potential_ext[:, 1:-1, 2:] - potential_ext[:, 1:-1, :-2]) * 0.5 * stretch
    north_slope = (potential_ext[:, 2:, 1:-1] - potential_ext[:, :-2, 1:-1]) * 0.5
    return (east_slope, north_slope)


def solve_cells(push_u, push_v, drag_field, wet_frac, coriolis):
    damping = drag_field + 4.0 * VISCOSITY
    frequency = jnp.array(FREQS, jnp.float32)[:, None, None]
    det_real = damping * damping - frequency * frequency + coriolis * coriolis
    det_imag = 2.0 * damping * frequency
    magnitude = det_real * det_real + det_imag * det_imag

    def combine(first, second, factor):
        top_real = damping * first[:6] - frequency * first[6:] + factor * coriolis * second[:6]
        top_imag = damping * first[6:] + frequency * first[:6] + factor * coriolis * second[6:]
        out_real = (top_real * det_real + top_imag * det_imag) / magnitude
        out_imag = (top_imag * det_real - top_real * det_imag) / magnitude
        return wet_frac * jnp.concatenate([out_real, out_imag], axis=0)

    return jnp.concatenate([combine(push_u, push_v, 1.0), combine(push_v, push_u, -1.0)], axis=0)


def inner(field, trim):
    return field[..., trim : field.shape[-2] - trim, trim : field.shape[-1] - trim]


def relax(flow_ext, east_slope, north_slope, depth_field, drag_field, wet_frac, coriolis):
    beside_all = (
        flow_ext[:, :-2, 1:-1]
        + flow_ext[:, 2:, 1:-1]
        + flow_ext[:, 1:-1, :-2]
        + flow_ext[:, 1:-1, 2:]
    )
    push_u = -depth_field * east_slope + VISCOSITY * beside_all[:12]
    push_v = -depth_field * north_slope + VISCOSITY * beside_all[12:]
    return solve_cells(push_u, push_v, drag_field, wet_frac, coriolis)


def surface(east_ext, north_ext, stretch, wet_frac):
    spread = (east_ext[:, :, 2:] - east_ext[:, :, :-2]) * 0.5 * stretch + (
        north_ext[:, 2:, :] - north_ext[:, :-2, :]
    ) * 0.5
    frequency = jnp.array(FREQS, jnp.float32)[:, None, None]
    return wet_frac * jnp.concatenate([-spread[6:] / frequency, spread[:6] / frequency], axis=0)


def per_device(
    elevation,
    equilibrium,
    transport_u,
    transport_v,
    ocean_depth,
    bottom_drag,
    wet_mask,
    lon_green,
    lat_green,
):
    rows_here = elevation.shape[1]
    total_rows = rows_here * lat_size()
    wet_frac = wet_mask.astype(jnp.float32)
    source = wet_frac * elevation
    mixed = jnp.einsum("krj,cj->krc", source, lon_green, precision=lax.Precision.HIGHEST)
    gathered = lax.all_gather(mixed, LAT, axis=1, tiled=True)

    fields = jnp.stack([ocean_depth, bottom_drag, wet_frac], axis=0)
    stack = jnp.concatenate([elevation - equilibrium, transport_u, transport_v, fields], axis=0)
    stack = widen_lat(widen_lon(stack, HALO, 2), HALO, 1)
    green_ext = widen_lat(lat_green, HALO, 0)

    columns = gathered.shape[2]
    size = lax.axis_size("lon")
    up = [(i, (i + 1) % size) for i in range(size)]
    down = [(j, i) for i, j in up]
    last = jnp.einsum(
        "rs,ksc->krc", green_ext, gathered[:, :, columns - HALO :], precision=lax.Precision.HIGHEST
    )
    initial = jnp.einsum(
        "rs,ksc->krc", green_ext, gathered[:, :, :HALO], precision=lax.Precision.HIGHEST
    )
    before = lax.ppermute(last, "lon", up)
    after = lax.ppermute(initial, "lon", down)
    sal = jnp.einsum("rs,ksc->krc", green_ext, gathered, precision=lax.Precision.HIGHEST)
    sal = jnp.concatenate([before, sal, after], axis=2)
    potential = stack[:12] - sal
    flows = stack[12:36]
    depth_ext, drag_ext, wet_ext = stack[36], stack[37], stack[38]

    first_row = lat_index() * rows_here - HALO
    stretch, coriolis = row_terms(first_row + jnp.arange(rows_here + 2 * HALO), total_rows)
    east_slope, north_slope = slopes(potential, stretch[1:-1])
    flows = relax(
        flows,
        east_slope,
        north_slope,
        inner(depth_ext, 1),
        inner(drag_ext, 1),
        inner(wet_ext, 1),
        coriolis[1:-1],
    )
    flows = relax(
        flows,
        inner(east_slope, 1),
        inner(north_slope, 1),
        inner(depth_ext, 2),
        inner(drag_ext, 2),
        inner(wet_ext, 2),
        coriolis[2:-2],
    )
    east_ext = flows[:12, 1:-1, :]
    north_ext = flows[12:, :, 1:-1]
    elevation_next = surface(east_ext, north_ext, stretch[HALO:-HALO], wet_frac)
    flows = inner(flows, 1)
    return (elevation_next, flows[:12], flows[12:])


def solution(mesh):
    lat_devices = mesh.shape["lat"]
    cores = 2 if lat_devices % 2 == 0 else 1
    devices = mesh.devices.reshape(mesh.shape["lon"], lat_devices // cores, cores)
    split = Mesh(devices, ("lon", "chip", "core"))
    grid = P(None, LAT, "lon")
    plane = P(LAT, "lon")
    placed = (grid, grid, grid, grid, plane, plane, plane, P("lon", None), plane)
    return jax.shard_map(
        per_device,
        mesh=split,
        in_specs=placed,
        out_specs=(grid, grid, grid),
        check_vma=False,
    )
```

```python
import math

import jax
import jax.numpy as jnp
from jax import lax
from jax.sharding import Mesh
from jax.sharding import PartitionSpec as P

FREQS = [1.9323, 2.0, 1.896, 2.0055, 1.0027, 0.9295]
VISCOSITY = 0.5
HALO = 3
LAT = ("chip", "core")


def lat_index():
    return lax.axis_index("chip") * lax.axis_size("core") + lax.axis_index("core")


def lat_size():
    return lax.axis_size("chip") * lax.axis_size("core")


def widen_lon(array, width, dim):
    size, length = lax.axis_size("lon"), array.shape[dim]
    up = [(i, (i + 1) % size) for i in range(size)]
    down = [(j, i) for i, j in up]
    last = lax.slice_in_dim(array, length - width, length, axis=dim)
    initial = lax.slice_in_dim(array, 0, width, axis=dim)
    before = lax.ppermute(last, "lon", up)
    after = lax.ppermute(initial, "lon", down)
    return jnp.concatenate([before, array, after], axis=dim)


def widen_lat(array, width, dim):
    size, length = lat_size(), array.shape[dim]
    up = [(i, i + 1) for i in range(size - 1)]
    down = [(j, i) for i, j in up]
    last = lax.slice_in_dim(array, length - width, length, axis=dim)
    initial = lax.slice_in_dim(array, 0, width, axis=dim)
    before = lax.ppermute(last, LAT, up)
    after = lax.ppermute(initial, LAT, down)
    return jnp.concatenate([before, array, after], axis=dim)


def row_terms(rows, nlat):
    angle = (-80.0 + 160.0 * (rows.astype(jnp.float32) + 0.5) / nlat) * (math.pi / 180.0)
    return ((1.0 / jnp.cos(angle))[:, None], (2.0 * jnp.sin(angle))[:, None])


def slopes(potential_ext, stretch):
    east_slope = (potential_ext[:, 1:-1, 2:] - potential_ext[:, 1:-1, :-2]) * 0.5 * stretch
    north_slope = (potential_ext[:, 2:, 1:-1] - potential_ext[:, :-2, 1:-1]) * 0.5
    return (east_slope, north_slope)


def solve_cells(push_u, push_v, drag_field, wet_frac, coriolis):
    damping = drag_field + 4.0 * VISCOSITY
    frequency = jnp.array(FREQS, jnp.float32)[:, None, None]
    det_real = damping * damping - frequency * frequency + coriolis * coriolis
    det_imag = 2.0 * damping * frequency
    magnitude = det_real * det_real + det_imag * det_imag

    def combine(first, second, factor):
        top_real = damping * first[:6] - frequency * first[6:] + factor * coriolis * second[:6]
        top_imag = damping * first[6:] + frequency * first[:6] + factor * coriolis * second[6:]
        out_real = (top_real * det_real + top_imag * det_imag) / magnitude
        out_imag = (top_imag * det_real - top_real * det_imag) / magnitude
        return wet_frac * jnp.concatenate([out_real, out_imag], axis=0)

    return jnp.concatenate([combine(push_u, push_v, 1.0), combine(push_v, push_u, -1.0)], axis=0)


def inner(field, trim):
    return field[..., trim : field.shape[-2] - trim, trim : field.shape[-1] - trim]


def relax(flow_ext, east_slope, north_slope, depth_field, drag_field, wet_frac, coriolis):
    beside_all = (
        flow_ext[:, :-2, 1:-1]
        + flow_ext[:, 2:, 1:-1]
        + flow_ext[:, 1:-1, :-2]
        + flow_ext[:, 1:-1, 2:]
    )
    push_u = -depth_field * east_slope + VISCOSITY * beside_all[:12]
    push_v = -depth_field * north_slope + VISCOSITY * beside_all[12:]
    return solve_cells(push_u, push_v, drag_field, wet_frac, coriolis)


def surface(east_ext, north_ext, stretch, wet_frac):
    spread = (east_ext[:, :, 2:] - east_ext[:, :, :-2]) * 0.5 * stretch + (
        north_ext[:, 2:, :] - north_ext[:, :-2, :]
    ) * 0.5
    frequency = jnp.array(FREQS, jnp.float32)[:, None, None]
    return wet_frac * jnp.concatenate([-spread[6:] / frequency, spread[:6] / frequency], axis=0)


def per_device(
    elevation,
    equilibrium,
    transport_u,
    transport_v,
    ocean_depth,
    bottom_drag,
    wet_mask,
    lon_green,
    lat_green,
):
    rows_here = elevation.shape[1]
    total_rows = rows_here * lat_size()
    wet_frac = wet_mask.astype(jnp.float32)
    source = wet_frac * elevation
    mixed = jnp.einsum("krj,cj->krc", source, lon_green, precision=lax.Precision.HIGHEST)
    columns = mixed.shape[2]
    edge_rows = jnp.concatenate([lon_green[:HALO], lon_green[columns - HALO :]], axis=0)
    edges = jnp.einsum("ej,krj->ker", edge_rows, source, precision=lax.Precision.HIGHEST)
    spare = 8 * ((2 * HALO + 7) // 8)
    edges = jnp.pad(edges, ((0, 0), (0, spare - 2 * HALO), (0, columns - rows_here)))
    packed = jnp.concatenate([mixed, edges], axis=1)
    gathered = lax.all_gather(packed, LAT, axis=1, tiled=True)

    fields = jnp.stack([ocean_depth, bottom_drag, wet_frac], axis=0)
    stack = jnp.concatenate([elevation - equilibrium, transport_u, transport_v, fields], axis=0)
    stack = widen_lat(widen_lon(stack, HALO, 2), HALO, 1)
    green_ext = widen_lat(lat_green, HALO, 0)

    blocks = lat_size()
    block = rows_here + spare
    green_blocks = green_ext.reshape(green_ext.shape[0], blocks, rows_here)
    lanes = gathered.reshape(12, blocks, block, columns)[:, :, rows_here : rows_here + 2 * HALO, :rows_here]
    edge_sal = jnp.einsum("rbj,kbej->kre", green_blocks, lanes, precision=lax.Precision.HIGHEST)
    size = lax.axis_size("lon")
    up = [(i, (i + 1) % size) for i in range(size)]
    down = [(j, i) for i, j in up]
    before = lax.ppermute(edge_sal[:, :, HALO:], "lon", up)
    after = lax.ppermute(edge_sal[:, :, :HALO], "lon", down)
    green_pad = jnp.pad(green_blocks, ((0, 0), (0, 0), (0, spare))).reshape(green_ext.shape[0], -1)
    sal = jnp.einsum("rs,ksc->krc", green_pad, gathered, precision=lax.Precision.HIGHEST)
    sal = jnp.concatenate([before, sal, after], axis=2)
    potential = stack[:12] - sal
    flows = stack[12:36]
    depth_ext, drag_ext, wet_ext = stack[36], stack[37], stack[38]

    first_row = lat_index() * rows_here - HALO
    stretch, coriolis = row_terms(first_row + jnp.arange(rows_here + 2 * HALO), total_rows)
    east_slope, north_slope = slopes(potential, stretch[1:-1])
    flows = relax(
        flows,
        east_slope,
        north_slope,
        inner(depth_ext, 1),
        inner(drag_ext, 1),
        inner(wet_ext, 1),
        coriolis[1:-1],
    )
    flows = relax(
        flows,
        inner(east_slope, 1),
        inner(north_slope, 1),
        inner(depth_ext, 2),
        inner(drag_ext, 2),
        inner(wet_ext, 2),
        coriolis[2:-2],
    )
    east_ext = flows[:12, 1:-1, :]
    north_ext = flows[12:, :, 1:-1]
    elevation_next = surface(east_ext, north_ext, stretch[HALO:-HALO], wet_frac)
    flows = inner(flows, 1)
    return (elevation_next, flows[:12], flows[12:])


def solution(mesh):
    lat_devices = mesh.shape["lat"]
    cores = 2 if lat_devices % 2 == 0 else 1
    devices = mesh.devices.reshape(mesh.shape["lon"], lat_devices // cores, cores)
    split = Mesh(devices, ("lon", "chip", "core"))
    grid = P(None, LAT, "lon")
    plane = P(LAT, "lon")
    placed = (grid, grid, grid, grid, plane, plane, plane, P("lon", None), plane)
    return jax.shard_map(
        per_device,
        mesh=split,
        in_specs=placed,
        out_specs=(grid, grid, grid),
        check_vma=False,
    )
```

```python
import math

import jax
import jax.numpy as jnp
from jax import lax
from jax.sharding import Mesh
from jax.sharding import PartitionSpec as P

FREQS = [1.9323, 2.0, 1.896, 2.0055, 1.0027, 0.9295]
VISCOSITY = 0.5
HALO = 3
LAT = ("chip", "core")


def lat_index():
    return lax.axis_index("chip") * lax.axis_size("core") + lax.axis_index("core")


def lat_size():
    return lax.axis_size("chip") * lax.axis_size("core")


def widen_lon(array, width, dim):
    size, length = lax.axis_size("lon"), array.shape[dim]
    up = [(i, (i + 1) % size) for i in range(size)]
    down = [(j, i) for i, j in up]
    last = lax.slice_in_dim(array, length - width, length, axis=dim)
    initial = lax.slice_in_dim(array, 0, width, axis=dim)
    before = lax.ppermute(last, "lon", up)
    after = lax.ppermute(initial, "lon", down)
    return jnp.concatenate([before, array, after], axis=dim)


def widen_lat(array, width, dim):
    size, length = lat_size(), array.shape[dim]
    up = [(i, i + 1) for i in range(size - 1)]
    down = [(j, i) for i, j in up]
    last = lax.slice_in_dim(array, length - width, length, axis=dim)
    initial = lax.slice_in_dim(array, 0, width, axis=dim)
    before = lax.ppermute(last, LAT, up)
    after = lax.ppermute(initial, LAT, down)
    return jnp.concatenate([before, array, after], axis=dim)


def row_terms(rows, nlat):
    angle = (-80.0 + 160.0 * (rows.astype(jnp.float32) + 0.5) / nlat) * (math.pi / 180.0)
    return ((1.0 / jnp.cos(angle))[:, None], (2.0 * jnp.sin(angle))[:, None])


def slopes(potential_ext, stretch):
    east_slope = (potential_ext[:, 1:-1, 2:] - potential_ext[:, 1:-1, :-2]) * 0.5 * stretch
    north_slope = (potential_ext[:, 2:, 1:-1] - potential_ext[:, :-2, 1:-1]) * 0.5
    return (east_slope, north_slope)


def solve_cells(push_u, push_v, drag_field, wet_frac, coriolis):
    damping = drag_field + 4.0 * VISCOSITY
    frequency = jnp.array(FREQS, jnp.float32)[:, None, None]
    det_real = damping * damping - frequency * frequency + coriolis * coriolis
    det_imag = 2.0 * damping * frequency
    magnitude = det_real * det_real + det_imag * det_imag

    def combine(first, second, factor):
        top_real = damping * first[:6] - frequency * first[6:] + factor * coriolis * second[:6]
        top_imag = damping * first[6:] + frequency * first[:6] + factor * coriolis * second[6:]
        out_real = (top_real * det_real + top_imag * det_imag) / magnitude
        out_imag = (top_imag * det_real - top_real * det_imag) / magnitude
        return wet_frac * jnp.concatenate([out_real, out_imag], axis=0)

    return jnp.concatenate([combine(push_u, push_v, 1.0), combine(push_v, push_u, -1.0)], axis=0)


def inner(field, trim):
    return field[..., trim : field.shape[-2] - trim, trim : field.shape[-1] - trim]


def relax(flow_ext, east_slope, north_slope, depth_field, drag_field, wet_frac, coriolis):
    beside_all = (
        flow_ext[:, :-2, 1:-1]
        + flow_ext[:, 2:, 1:-1]
        + flow_ext[:, 1:-1, :-2]
        + flow_ext[:, 1:-1, 2:]
    )
    push_u = -depth_field * east_slope + VISCOSITY * beside_all[:12]
    push_v = -depth_field * north_slope + VISCOSITY * beside_all[12:]
    return solve_cells(push_u, push_v, drag_field, wet_frac, coriolis)


def surface(east_ext, north_ext, stretch, wet_frac):
    spread = (east_ext[:, :, 2:] - east_ext[:, :, :-2]) * 0.5 * stretch + (
        north_ext[:, 2:, :] - north_ext[:, :-2, :]
    ) * 0.5
    frequency = jnp.array(FREQS, jnp.float32)[:, None, None]
    return wet_frac * jnp.concatenate([-spread[6:] / frequency, spread[:6] / frequency], axis=0)


def per_device(
    elevation,
    equilibrium,
    transport_u,
    transport_v,
    ocean_depth,
    bottom_drag,
    wet_mask,
    lon_green,
    lat_green,
):
    rows_here = elevation.shape[1]
    total_rows = rows_here * lat_size()
    wet_frac = wet_mask.astype(jnp.float32)
    source = wet_frac * elevation
    mixed = jnp.einsum("krj,cj->krc", source, lon_green, precision=lax.Precision.HIGHEST)
    gathered = lax.all_gather(mixed, LAT, axis=1, tiled=True)

    fields = jnp.stack([ocean_depth, bottom_drag, wet_frac], axis=0)
    stack = jnp.concatenate([elevation - equilibrium, transport_u, transport_v, fields], axis=0)
    stack = widen_lat(widen_lon(stack, HALO, 2), HALO, 1)
    green_ext = widen_lat(lat_green, HALO, 0)

    columns = mixed.shape[2]
    edge_rows = jnp.concatenate([lon_green[:HALO], lon_green[columns - HALO :]], axis=0)
    edges = jnp.einsum("ej,krj->ker", edge_rows, source, precision=lax.Precision.HIGHEST)
    size = lax.axis_size("lon")
    up = [(i, (i + 1) % size) for i in range(size)]
    down = [(j, i) for i, j in up]
    near_edges = jnp.concatenate(
        [lax.ppermute(edges[:, HALO:], "lon", up), lax.ppermute(edges[:, :HALO], "lon", down)], axis=1
    )
    near_edges = lax.all_gather(near_edges, LAT, axis=2, tiled=True)
    green_before = lax.ppermute(green_ext, "lon", up)
    green_after = lax.ppermute(green_ext, "lon", down)
    sal = jnp.einsum("rs,ksc->krc", green_ext, gathered, precision=lax.Precision.HIGHEST)
    sal_before = jnp.einsum(
        "rs,kes->kre", green_before, near_edges[:, :HALO], precision=lax.Precision.HIGHEST
    )
    sal_after = jnp.einsum(
        "rs,kes->kre", green_after, near_edges[:, HALO:], precision=lax.Precision.HIGHEST
    )
    sal = jnp.concatenate([sal_before, sal, sal_after], axis=2)
    potential = stack[:12] - sal
    flows = stack[12:36]
    depth_ext, drag_ext, wet_ext = stack[36], stack[37], stack[38]

    first_row = lat_index() * rows_here - HALO
    stretch, coriolis = row_terms(first_row + jnp.arange(rows_here + 2 * HALO), total_rows)
    east_slope, north_slope = slopes(potential, stretch[1:-1])
    flows = relax(
        flows,
        east_slope,
        north_slope,
        inner(depth_ext, 1),
        inner(drag_ext, 1),
        inner(wet_ext, 1),
        coriolis[1:-1],
    )
    flows = relax(
        flows,
        inner(east_slope, 1),
        inner(north_slope, 1),
        inner(depth_ext, 2),
        inner(drag_ext, 2),
        inner(wet_ext, 2),
        coriolis[2:-2],
    )
    east_ext = flows[:12, 1:-1, :]
    north_ext = flows[12:, :, 1:-1]
    elevation_next = surface(east_ext, north_ext, stretch[HALO:-HALO], wet_frac)
    flows = inner(flows, 1)
    return (elevation_next, flows[:12], flows[12:])


def solution(mesh):
    lat_devices = mesh.shape["lat"]
    cores = 2 if lat_devices % 2 == 0 else 1
    devices = mesh.devices.reshape(mesh.shape["lon"], lat_devices // cores, cores)
    split = Mesh(devices, ("lon", "chip", "core"))
    grid = P(None, LAT, "lon")
    plane = P(LAT, "lon")
    placed = (grid, grid, grid, grid, plane, plane, plane, P("lon", None), plane)
    return jax.shard_map(
        per_device,
        mesh=split,
        in_specs=placed,
        out_specs=(grid, grid, grid),
        check_vma=False,
    )
```

```python
import math

import jax
import jax.numpy as jnp
from jax import lax
from jax.sharding import Mesh
from jax.sharding import PartitionSpec as P

FREQS = [1.9323, 2.0, 1.896, 2.0055, 1.0027, 0.9295]
VISCOSITY = 0.5
HALO = 3
LAT = ("chip", "core")


def lat_index():
    return lax.axis_index("chip") * lax.axis_size("core") + lax.axis_index("core")


def lat_size():
    return lax.axis_size("chip") * lax.axis_size("core")


def widen_lon(array, width, dim):
    size, length = lax.axis_size("lon"), array.shape[dim]
    up = [(i, (i + 1) % size) for i in range(size)]
    down = [(j, i) for i, j in up]
    last = lax.slice_in_dim(array, length - width, length, axis=dim)
    initial = lax.slice_in_dim(array, 0, width, axis=dim)
    before = lax.ppermute(last, "lon", up)
    after = lax.ppermute(initial, "lon", down)
    return jnp.concatenate([before, array, after], axis=dim)


def widen_lat(array, width, dim):
    size, length = lat_size(), array.shape[dim]
    up = [(i, i + 1) for i in range(size - 1)]
    down = [(j, i) for i, j in up]
    last = lax.slice_in_dim(array, length - width, length, axis=dim)
    initial = lax.slice_in_dim(array, 0, width, axis=dim)
    before = lax.ppermute(last, LAT, up)
    after = lax.ppermute(initial, LAT, down)
    return jnp.concatenate([before, array, after], axis=dim)


def row_terms(rows, nlat):
    angle = (-80.0 + 160.0 * (rows.astype(jnp.float32) + 0.5) / nlat) * (math.pi / 180.0)
    return ((1.0 / jnp.cos(angle))[:, None], (2.0 * jnp.sin(angle))[:, None])


def slopes(potential_ext, stretch):
    east_slope = (potential_ext[:, 1:-1, 2:] - potential_ext[:, 1:-1, :-2]) * 0.5 * stretch
    north_slope = (potential_ext[:, 2:, 1:-1] - potential_ext[:, :-2, 1:-1]) * 0.5
    return (east_slope, north_slope)


def solve_cells(push_u, push_v, drag_field, wet_frac, coriolis):
    damping = drag_field + 4.0 * VISCOSITY
    frequency = jnp.array(FREQS, jnp.float32)[:, None, None]
    det_real = damping * damping - frequency * frequency + coriolis * coriolis
    det_imag = 2.0 * damping * frequency
    magnitude = det_real * det_real + det_imag * det_imag

    def combine(first, second, factor):
        top_real = damping * first[:6] - frequency * first[6:] + factor * coriolis * second[:6]
        top_imag = damping * first[6:] + frequency * first[:6] + factor * coriolis * second[6:]
        out_real = (top_real * det_real + top_imag * det_imag) / magnitude
        out_imag = (top_imag * det_real - top_real * det_imag) / magnitude
        return wet_frac * jnp.concatenate([out_real, out_imag], axis=0)

    return jnp.concatenate([combine(push_u, push_v, 1.0), combine(push_v, push_u, -1.0)], axis=0)


def inner(field, trim):
    return field[..., trim : field.shape[-2] - trim, trim : field.shape[-1] - trim]


def relax(flow_ext, east_slope, north_slope, depth_field, drag_field, wet_frac, coriolis):
    beside_all = (
        flow_ext[:, :-2, 1:-1]
        + flow_ext[:, 2:, 1:-1]
        + flow_ext[:, 1:-1, :-2]
        + flow_ext[:, 1:-1, 2:]
    )
    push_u = -depth_field * east_slope + VISCOSITY * beside_all[:12]
    push_v = -depth_field * north_slope + VISCOSITY * beside_all[12:]
    return solve_cells(push_u, push_v, drag_field, wet_frac, coriolis)


def surface(east_ext, north_ext, stretch, wet_frac):
    spread = (east_ext[:, :, 2:] - east_ext[:, :, :-2]) * 0.5 * stretch + (
        north_ext[:, 2:, :] - north_ext[:, :-2, :]
    ) * 0.5
    frequency = jnp.array(FREQS, jnp.float32)[:, None, None]
    return wet_frac * jnp.concatenate([-spread[6:] / frequency, spread[:6] / frequency], axis=0)


def per_device(
    elevation,
    equilibrium,
    transport_u,
    transport_v,
    ocean_depth,
    bottom_drag,
    wet_mask,
    lon_green,
    lat_green,
):
    rows_here = elevation.shape[1]
    total_rows = rows_here * lat_size()
    wet_frac = wet_mask.astype(jnp.float32)
    source = wet_frac * elevation
    mixed = jnp.einsum("krj,cj->krc", source, lon_green, precision=lax.Precision.HIGHEST)
    columns = mixed.shape[2]
    edge_rows = jnp.concatenate([lon_green[:HALO], lon_green[columns - HALO :]], axis=0)
    edges = jnp.einsum("ej,krj->ker", edge_rows, source, precision=lax.Precision.HIGHEST)
    spare = 8 * ((2 * HALO + 7) // 8)
    edges = jnp.pad(edges, ((0, 0), (0, spare - 2 * HALO), (0, columns - rows_here)))
    packed = jnp.concatenate([mixed, edges], axis=1)
    gathered = lax.all_gather(packed, "chip", axis=1, tiled=True)
    cores = lax.axis_size("core")
    core = lax.axis_index("core")
    swap = [(i, (i + 1) % cores) for i in range(cores)]

    fields = jnp.stack([ocean_depth, bottom_drag, wet_frac], axis=0)
    stack = jnp.concatenate([elevation - equilibrium, transport_u, transport_v, fields], axis=0)
    stack = widen_lat(widen_lon(stack, HALO, 2), HALO, 1)
    green_ext = widen_lat(lat_green, HALO, 0)
    gathered, stack, green_ext = lax.optimization_barrier((gathered, stack, green_ext))

    swapped = lax.ppermute(gathered, "core", swap)
    chips = lax.axis_size("chip")
    block = rows_here + spare
    ext_rows = green_ext.shape[0]
    green_blocks = green_ext.reshape(ext_rows, chips, cores, rows_here)
    green_own = lax.dynamic_index_in_dim(green_blocks, core, axis=2, keepdims=False)
    green_other = lax.dynamic_index_in_dim(green_blocks, (core + 1) % cores, axis=2, keepdims=False)

    def edge_part(green_part, part):
        lanes = part.reshape(12, chips, block, columns)[:, :, rows_here : rows_here + 2 * HALO, :rows_here]
        return jnp.einsum("rbj,kbej->kre", green_part, lanes, precision=lax.Precision.HIGHEST)

    def bulk_part(green_part, part):
        padded = jnp.pad(green_part, ((0, 0), (0, 0), (0, spare))).reshape(ext_rows, -1)
        return jnp.einsum("rs,ksc->krc", padded, part, precision=lax.Precision.HIGHEST)

    edge_own = edge_part(green_own, gathered)
    sal_own = bulk_part(green_own, gathered)
    edge_sal = edge_own + edge_part(green_other, swapped)
    size = lax.axis_size("lon")
    up = [(i, (i + 1) % size) for i in range(size)]
    down = [(j, i) for i, j in up]
    before = lax.ppermute(edge_sal[:, :, HALO:], "lon", up)
    after = lax.ppermute(edge_sal[:, :, :HALO], "lon", down)
    sal = sal_own + bulk_part(green_other, swapped)
    sal = jnp.concatenate([before, sal, after], axis=2)
    potential = stack[:12] - sal
    flows = stack[12:36]
    depth_ext, drag_ext, wet_ext = stack[36], stack[37], stack[38]

    first_row = lat_index() * rows_here - HALO
    stretch, coriolis = row_terms(first_row + jnp.arange(rows_here + 2 * HALO), total_rows)
    east_slope, north_slope = slopes(potential, stretch[1:-1])
    flows = relax(
        flows,
        east_slope,
        north_slope,
        inner(depth_ext, 1),
        inner(drag_ext, 1),
        inner(wet_ext, 1),
        coriolis[1:-1],
    )
    flows = relax(
        flows,
        inner(east_slope, 1),
        inner(north_slope, 1),
        inner(depth_ext, 2),
        inner(drag_ext, 2),
        inner(wet_ext, 2),
        coriolis[2:-2],
    )
    east_ext = flows[:12, 1:-1, :]
    north_ext = flows[12:, :, 1:-1]
    elevation_next = surface(east_ext, north_ext, stretch[HALO:-HALO], wet_frac)
    flows = inner(flows, 1)
    return (elevation_next, flows[:12], flows[12:])


def solution(mesh):
    lat_devices = mesh.shape["lat"]
    cores = 2 if lat_devices % 2 == 0 else 1
    devices = mesh.devices.reshape(mesh.shape["lon"], lat_devices // cores, cores)
    split = Mesh(devices, ("lon", "chip", "core"))
    grid = P(None, LAT, "lon")
    plane = P(LAT, "lon")
    placed = (grid, grid, grid, grid, plane, plane, plane, P("lon", None), plane)
    return jax.shard_map(
        per_device,
        mesh=split,
        in_specs=placed,
        out_specs=(grid, grid, grid),
        check_vma=False,
    )
```

```python
import math

import jax
import jax.numpy as jnp
from jax import lax
from jax.sharding import Mesh
from jax.sharding import PartitionSpec as P

FREQS = [1.9323, 2.0, 1.896, 2.0055, 1.0027, 0.9295]
VISCOSITY = 0.5
HALO = 3
LAT = ("chip", "core")


def lat_index():
    return lax.axis_index("chip") * lax.axis_size("core") + lax.axis_index("core")


def lat_size():
    return lax.axis_size("chip") * lax.axis_size("core")


def widen_lon(array, width, dim):
    size, length = lax.axis_size("lon"), array.shape[dim]
    up = [(i, (i + 1) % size) for i in range(size)]
    down = [(j, i) for i, j in up]
    last = lax.slice_in_dim(array, length - width, length, axis=dim)
    initial = lax.slice_in_dim(array, 0, width, axis=dim)
    before = lax.ppermute(last, "lon", up)
    after = lax.ppermute(initial, "lon", down)
    return jnp.concatenate([before, array, after], axis=dim)


def widen_lat(array, width, dim):
    size, length = lat_size(), array.shape[dim]
    up = [(i, i + 1) for i in range(size - 1)]
    down = [(j, i) for i, j in up]
    last = lax.slice_in_dim(array, length - width, length, axis=dim)
    initial = lax.slice_in_dim(array, 0, width, axis=dim)
    before = lax.ppermute(last, LAT, up)
    after = lax.ppermute(initial, LAT, down)
    return jnp.concatenate([before, array, after], axis=dim)


def row_terms(rows, nlat):
    angle = (-80.0 + 160.0 * (rows.astype(jnp.float32) + 0.5) / nlat) * (math.pi / 180.0)
    return ((1.0 / jnp.cos(angle))[:, None], (2.0 * jnp.sin(angle))[:, None])


def slopes(potential_ext, stretch):
    east_slope = (potential_ext[:, 1:-1, 2:] - potential_ext[:, 1:-1, :-2]) * 0.5 * stretch
    north_slope = (potential_ext[:, 2:, 1:-1] - potential_ext[:, :-2, 1:-1]) * 0.5
    return (east_slope, north_slope)


def solve_cells(push_u, push_v, drag_field, wet_frac, coriolis):
    damping = drag_field + 4.0 * VISCOSITY
    frequency = jnp.array(FREQS, jnp.float32)[:, None, None]
    det_real = damping * damping - frequency * frequency + coriolis * coriolis
    det_imag = 2.0 * damping * frequency
    magnitude = det_real * det_real + det_imag * det_imag

    def combine(first, second, factor):
        top_real = damping * first[:6] - frequency * first[6:] + factor * coriolis * second[:6]
        top_imag = damping * first[6:] + frequency * first[:6] + factor * coriolis * second[6:]
        out_real = (top_real * det_real + top_imag * det_imag) / magnitude
        out_imag = (top_imag * det_real - top_real * det_imag) / magnitude
        return wet_frac * jnp.concatenate([out_real, out_imag], axis=0)

    return jnp.concatenate([combine(push_u, push_v, 1.0), combine(push_v, push_u, -1.0)], axis=0)


def inner(field, trim):
    return field[..., trim : field.shape[-2] - trim, trim : field.shape[-1] - trim]


def relax(flow_ext, east_slope, north_slope, depth_field, drag_field, wet_frac, coriolis):
    beside_all = (
        flow_ext[:, :-2, 1:-1]
        + flow_ext[:, 2:, 1:-1]
        + flow_ext[:, 1:-1, :-2]
        + flow_ext[:, 1:-1, 2:]
    )
    push_u = -depth_field * east_slope + VISCOSITY * beside_all[:12]
    push_v = -depth_field * north_slope + VISCOSITY * beside_all[12:]
    return solve_cells(push_u, push_v, drag_field, wet_frac, coriolis)


def surface(east_ext, north_ext, stretch, wet_frac):
    spread = (east_ext[:, :, 2:] - east_ext[:, :, :-2]) * 0.5 * stretch + (
        north_ext[:, 2:, :] - north_ext[:, :-2, :]
    ) * 0.5
    frequency = jnp.array(FREQS, jnp.float32)[:, None, None]
    return wet_frac * jnp.concatenate([-spread[6:] / frequency, spread[:6] / frequency], axis=0)


def per_device(
    elevation,
    equilibrium,
    transport_u,
    transport_v,
    ocean_depth,
    bottom_drag,
    wet_mask,
    lon_green,
    lat_green,
):
    rows_here = elevation.shape[1]
    total_rows = rows_here * lat_size()
    wet_frac = wet_mask.astype(jnp.float32)
    source = wet_frac * elevation
    mixed = jnp.einsum("krj,cj->krc", source, lon_green, precision=lax.Precision.HIGHEST)
    columns = mixed.shape[2]
    edge_rows = jnp.concatenate([lon_green[:HALO], lon_green[columns - HALO :]], axis=0)
    edges = jnp.einsum("ej,krj->ker", edge_rows, source, precision=lax.Precision.HIGHEST)
    spare = 8 * ((2 * HALO + 7) // 8)
    edges = jnp.pad(edges, ((0, 0), (0, spare - 2 * HALO), (0, columns - rows_here)))
    packed = jnp.concatenate([mixed, edges], axis=1)
    gathered = lax.all_gather(packed, LAT, axis=1, tiled=True)

    fields = jnp.stack([ocean_depth, bottom_drag, wet_frac], axis=0)
    stack = jnp.concatenate([elevation - equilibrium, transport_u, transport_v, fields], axis=0)
    stack = widen_lat(widen_lon(stack, HALO, 2), HALO, 1)
    green_ext = widen_lat(lat_green, HALO, 0)

    blocks = lat_size()
    block = rows_here + spare
    green_blocks = green_ext.reshape(green_ext.shape[0], blocks, rows_here)
    lanes = gathered.reshape(12, blocks, block, columns)[:, :, rows_here : rows_here + 2 * HALO, :rows_here]
    edge_sal = jnp.einsum("rbj,kbej->kre", green_blocks, lanes, precision=lax.Precision.HIGHEST)
    size = lax.axis_size("lon")
    up = [(i, (i + 1) % size) for i in range(size)]
    down = [(j, i) for i, j in up]
    green_pad = jnp.pad(green_blocks, ((0, 0), (0, 0), (0, spare))).reshape(green_ext.shape[0], -1)
    sal = jnp.einsum("rs,ksc->krc", green_pad, gathered, precision=lax.Precision.HIGHEST)
    edge_sal, sal = lax.optimization_barrier((edge_sal, sal))
    before = lax.ppermute(edge_sal[:, :, HALO:], "lon", up)
    after = lax.ppermute(edge_sal[:, :, :HALO], "lon", down)
    sal = jnp.concatenate([before, sal, after], axis=2)
    potential = stack[:12] - sal
    flows = stack[12:36]
    depth_ext, drag_ext, wet_ext = stack[36], stack[37], stack[38]

    first_row = lat_index() * rows_here - HALO
    stretch, coriolis = row_terms(first_row + jnp.arange(rows_here + 2 * HALO), total_rows)
    east_slope, north_slope = slopes(potential, stretch[1:-1])
    flows = relax(
        flows,
        east_slope,
        north_slope,
        inner(depth_ext, 1),
        inner(drag_ext, 1),
        inner(wet_ext, 1),
        coriolis[1:-1],
    )
    flows = relax(
        flows,
        inner(east_slope, 1),
        inner(north_slope, 1),
        inner(depth_ext, 2),
        inner(drag_ext, 2),
        inner(wet_ext, 2),
        coriolis[2:-2],
    )
    east_ext = flows[:12, 1:-1, :]
    north_ext = flows[12:, :, 1:-1]
    elevation_next = surface(east_ext, north_ext, stretch[HALO:-HALO], wet_frac)
    flows = inner(flows, 1)
    return (elevation_next, flows[:12], flows[12:])


def solution(mesh):
    lat_devices = mesh.shape["lat"]
    cores = 2 if lat_devices % 2 == 0 else 1
    devices = mesh.devices.reshape(mesh.shape["lon"], lat_devices // cores, cores)
    split = Mesh(devices, ("lon", "chip", "core"))
    grid = P(None, LAT, "lon")
    plane = P(LAT, "lon")
    placed = (grid, grid, grid, grid, plane, plane, plane, P("lon", None), plane)
    return jax.shard_map(
        per_device,
        mesh=split,
        in_specs=placed,
        out_specs=(grid, grid, grid),
        check_vma=False,
    )
```

```python
import math

import jax
import jax.numpy as jnp
from jax import lax
from jax.sharding import Mesh
from jax.sharding import PartitionSpec as P

FREQS = [1.9323, 2.0, 1.896, 2.0055, 1.0027, 0.9295]
VISCOSITY = 0.5
HALO = 3
LAT = ("chip", "core")


def lat_index():
    return lax.axis_index("chip") * lax.axis_size("core") + lax.axis_index("core")


def lat_size():
    return lax.axis_size("chip") * lax.axis_size("core")


def widen_lon(array, width, dim):
    size, length = lax.axis_size("lon"), array.shape[dim]
    up = [(i, (i + 1) % size) for i in range(size)]
    down = [(j, i) for i, j in up]
    last = lax.slice_in_dim(array, length - width, length, axis=dim)
    initial = lax.slice_in_dim(array, 0, width, axis=dim)
    before = lax.ppermute(last, "lon", up)
    after = lax.ppermute(initial, "lon", down)
    return jnp.concatenate([before, array, after], axis=dim)


def widen_lat(array, width, dim):
    size, length = lat_size(), array.shape[dim]
    up = [(i, i + 1) for i in range(size - 1)]
    down = [(j, i) for i, j in up]
    last = lax.slice_in_dim(array, length - width, length, axis=dim)
    initial = lax.slice_in_dim(array, 0, width, axis=dim)
    before = lax.ppermute(last, LAT, up)
    after = lax.ppermute(initial, LAT, down)
    return jnp.concatenate([before, array, after], axis=dim)


def row_terms(rows, nlat):
    angle = (-80.0 + 160.0 * (rows.astype(jnp.float32) + 0.5) / nlat) * (math.pi / 180.0)
    return ((1.0 / jnp.cos(angle))[:, None], (2.0 * jnp.sin(angle))[:, None])


def slopes(potential_ext, stretch):
    east_slope = (potential_ext[:, 1:-1, 2:] - potential_ext[:, 1:-1, :-2]) * 0.5 * stretch
    north_slope = (potential_ext[:, 2:, 1:-1] - potential_ext[:, :-2, 1:-1]) * 0.5
    return (east_slope, north_slope)


def solve_cells(push_u, push_v, drag_field, wet_frac, coriolis):
    damping = drag_field + 4.0 * VISCOSITY
    frequency = jnp.array(FREQS, jnp.float32)[:, None, None]
    det_real = damping * damping - frequency * frequency + coriolis * coriolis
    det_imag = 2.0 * damping * frequency
    magnitude = det_real * det_real + det_imag * det_imag

    def combine(first, second, factor):
        top_real = damping * first[:6] - frequency * first[6:] + factor * coriolis * second[:6]
        top_imag = damping * first[6:] + frequency * first[:6] + factor * coriolis * second[6:]
        out_real = (top_real * det_real + top_imag * det_imag) / magnitude
        out_imag = (top_imag * det_real - top_real * det_imag) / magnitude
        return wet_frac * jnp.concatenate([out_real, out_imag], axis=0)

    return jnp.concatenate([combine(push_u, push_v, 1.0), combine(push_v, push_u, -1.0)], axis=0)


def inner(field, trim):
    return field[..., trim : field.shape[-2] - trim, trim : field.shape[-1] - trim]


def relax(flow_ext, east_slope, north_slope, depth_field, drag_field, wet_frac, coriolis):
    beside_all = (
        flow_ext[:, :-2, 1:-1]
        + flow_ext[:, 2:, 1:-1]
        + flow_ext[:, 1:-1, :-2]
        + flow_ext[:, 1:-1, 2:]
    )
    push_u = -depth_field * east_slope + VISCOSITY * beside_all[:12]
    push_v = -depth_field * north_slope + VISCOSITY * beside_all[12:]
    return solve_cells(push_u, push_v, drag_field, wet_frac, coriolis)


def surface(east_ext, north_ext, stretch, wet_frac):
    spread = (east_ext[:, :, 2:] - east_ext[:, :, :-2]) * 0.5 * stretch + (
        north_ext[:, 2:, :] - north_ext[:, :-2, :]
    ) * 0.5
    frequency = jnp.array(FREQS, jnp.float32)[:, None, None]
    return wet_frac * jnp.concatenate([-spread[6:] / frequency, spread[:6] / frequency], axis=0)


def per_device(
    elevation,
    equilibrium,
    transport_u,
    transport_v,
    ocean_depth,
    bottom_drag,
    wet_mask,
    lon_green,
    lat_green,
):
    rows_here = elevation.shape[1]
    total_rows = rows_here * lat_size()
    wet_frac = wet_mask.astype(jnp.float32)
    source = wet_frac * elevation
    mixed = jnp.einsum("krj,cj->krc", source, lon_green, precision=lax.Precision.HIGHEST)
    columns = mixed.shape[2]
    edge_rows = jnp.concatenate([lon_green[:HALO], lon_green[columns - HALO :]], axis=0)
    edges = jnp.einsum("ej,krj->ker", edge_rows, source, precision=lax.Precision.HIGHEST)
    size = lax.axis_size("lon")
    up = [(i, (i + 1) % size) for i in range(size)]
    down = [(j, i) for i, j in up]
    edges = jnp.concatenate(
        [lax.ppermute(edges[:, HALO:], "lon", up), lax.ppermute(edges[:, :HALO], "lon", down)], axis=1
    )
    spare = 8 * ((2 * HALO + 7) // 8)
    edges = jnp.pad(edges, ((0, 0), (0, spare - 2 * HALO), (0, columns - rows_here)))
    packed = jnp.concatenate([mixed, edges], axis=1)
    gathered = lax.all_gather(packed, LAT, axis=1, tiled=True)

    fields = jnp.stack([ocean_depth, bottom_drag, wet_frac], axis=0)
    stack = jnp.concatenate([elevation - equilibrium, transport_u, transport_v, fields], axis=0)
    stack = widen_lat(widen_lon(stack, HALO, 2), HALO, 1)
    green_ext = widen_lat(lat_green, HALO, 0)

    blocks = lat_size()
    block = rows_here + spare
    green_blocks = green_ext.reshape(green_ext.shape[0], blocks, rows_here)
    lanes = gathered.reshape(12, blocks, block, columns)[:, :, rows_here : rows_here + 2 * HALO, :rows_here]
    green_before = lax.ppermute(green_blocks, "lon", up)
    green_after = lax.ppermute(green_blocks, "lon", down)
    before = jnp.einsum(
        "rbj,kbej->kre", green_before, lanes[:, :, :HALO], precision=lax.Precision.HIGHEST
    )
    after = jnp.einsum(
        "rbj,kbej->kre", green_after, lanes[:, :, HALO:], precision=lax.Precision.HIGHEST
    )
    green_pad = jnp.pad(green_blocks, ((0, 0), (0, 0), (0, spare))).reshape(green_ext.shape[0], -1)
    sal = jnp.einsum("rs,ksc->krc", green_pad, gathered, precision=lax.Precision.HIGHEST)
    sal = jnp.concatenate([before, sal, after], axis=2)
    potential = stack[:12] - sal
    flows = stack[12:36]
    depth_ext, drag_ext, wet_ext = stack[36], stack[37], stack[38]

    first_row = lat_index() * rows_here - HALO
    stretch, coriolis = row_terms(first_row + jnp.arange(rows_here + 2 * HALO), total_rows)
    east_slope, north_slope = slopes(potential, stretch[1:-1])
    flows = relax(
        flows,
        east_slope,
        north_slope,
        inner(depth_ext, 1),
        inner(drag_ext, 1),
        inner(wet_ext, 1),
        coriolis[1:-1],
    )
    flows = relax(
        flows,
        inner(east_slope, 1),
        inner(north_slope, 1),
        inner(depth_ext, 2),
        inner(drag_ext, 2),
        inner(wet_ext, 2),
        coriolis[2:-2],
    )
    east_ext = flows[:12, 1:-1, :]
    north_ext = flows[12:, :, 1:-1]
    elevation_next = surface(east_ext, north_ext, stretch[HALO:-HALO], wet_frac)
    flows = inner(flows, 1)
    return (elevation_next, flows[:12], flows[12:])


def solution(mesh):
    lat_devices = mesh.shape["lat"]
    cores = 2 if lat_devices % 2 == 0 else 1
    devices = mesh.devices.reshape(mesh.shape["lon"], lat_devices // cores, cores)
    split = Mesh(devices, ("lon", "chip", "core"))
    grid = P(None, LAT, "lon")
    plane = P(LAT, "lon")
    placed = (grid, grid, grid, grid, plane, plane, plane, P("lon", None), plane)
    return jax.shard_map(
        per_device,
        mesh=split,
        in_specs=placed,
        out_specs=(grid, grid, grid),
        check_vma=False,
    )
```

```python
import math

import jax
import jax.numpy as jnp
from jax import lax
from jax.sharding import Mesh
from jax.sharding import PartitionSpec as P

FREQS = [1.9323, 2.0, 1.896, 2.0055, 1.0027, 0.9295]
VISCOSITY = 0.5
HALO = 3
LAT = ("chip", "core")
STREAMS = ((0, 1, 2), (3, 4, 5))


def lat_index():
    return lax.axis_index("chip") * lax.axis_size("core") + lax.axis_index("core")


def lat_size():
    return lax.axis_size("chip") * lax.axis_size("core")


def widen_lon(array, width, dim):
    size, length = lax.axis_size("lon"), array.shape[dim]
    up = [(i, (i + 1) % size) for i in range(size)]
    down = [(j, i) for i, j in up]
    last = lax.slice_in_dim(array, length - width, length, axis=dim)
    initial = lax.slice_in_dim(array, 0, width, axis=dim)
    before = lax.ppermute(last, "lon", up)
    after = lax.ppermute(initial, "lon", down)
    return jnp.concatenate([before, array, after], axis=dim)


def widen_lat(array, width, dim):
    size, length = lat_size(), array.shape[dim]
    up = [(i, i + 1) for i in range(size - 1)]
    down = [(j, i) for i, j in up]
    last = lax.slice_in_dim(array, length - width, length, axis=dim)
    initial = lax.slice_in_dim(array, 0, width, axis=dim)
    before = lax.ppermute(last, LAT, up)
    after = lax.ppermute(initial, LAT, down)
    return jnp.concatenate([before, array, after], axis=dim)


def row_terms(rows, nlat):
    angle = (-80.0 + 160.0 * (rows.astype(jnp.float32) + 0.5) / nlat) * (math.pi / 180.0)
    return ((1.0 / jnp.cos(angle))[:, None], (2.0 * jnp.sin(angle))[:, None])


def slopes(potential_ext, stretch):
    east_slope = (potential_ext[:, 1:-1, 2:] - potential_ext[:, 1:-1, :-2]) * 0.5 * stretch
    north_slope = (potential_ext[:, 2:, 1:-1] - potential_ext[:, :-2, 1:-1]) * 0.5
    return (east_slope, north_slope)


def solve_cells(push_u, push_v, drag_field, wet_frac, coriolis, freqs):
    n = len(freqs)
    damping = drag_field + 4.0 * VISCOSITY
    frequency = jnp.array(freqs, jnp.float32)[:, None, None]
    det_real = damping * damping - frequency * frequency + coriolis * coriolis
    det_imag = 2.0 * damping * frequency
    magnitude = det_real * det_real + det_imag * det_imag

    def combine(first, second, factor):
        top_real = damping * first[:n] - frequency * first[n:] + factor * coriolis * second[:n]
        top_imag = damping * first[n:] + frequency * first[:n] + factor * coriolis * second[n:]
        out_real = (top_real * det_real + top_imag * det_imag) / magnitude
        out_imag = (top_imag * det_real - top_real * det_imag) / magnitude
        return wet_frac * jnp.concatenate([out_real, out_imag], axis=0)

    return jnp.concatenate([combine(push_u, push_v, 1.0), combine(push_v, push_u, -1.0)], axis=0)


def inner(field, trim):
    return field[..., trim : field.shape[-2] - trim, trim : field.shape[-1] - trim]


def relax(flow_ext, east_slope, north_slope, depth_field, drag_field, wet_frac, coriolis, freqs):
    half = 2 * len(freqs)
    beside_all = (
        flow_ext[:, :-2, 1:-1]
        + flow_ext[:, 2:, 1:-1]
        + flow_ext[:, 1:-1, :-2]
        + flow_ext[:, 1:-1, 2:]
    )
    push_u = -depth_field * east_slope + VISCOSITY * beside_all[:half]
    push_v = -depth_field * north_slope + VISCOSITY * beside_all[half:]
    return solve_cells(push_u, push_v, drag_field, wet_frac, coriolis, freqs)


def surface(east_ext, north_ext, stretch, wet_frac, freqs):
    n = len(freqs)
    spread = (east_ext[:, :, 2:] - east_ext[:, :, :-2]) * 0.5 * stretch + (
        north_ext[:, 2:, :] - north_ext[:, :-2, :]
    ) * 0.5
    frequency = jnp.array(freqs, jnp.float32)[:, None, None]
    return wet_frac * jnp.concatenate([-spread[n:] / frequency, spread[:n] / frequency], axis=0)


def pick(array, start, stream):
    low, high = stream[0], stream[-1] + 1
    return jnp.concatenate(
        [array[start + low : start + high], array[start + 6 + low : start + 6 + high]], axis=0
    )


def per_device(
    elevation,
    equilibrium,
    transport_u,
    transport_v,
    ocean_depth,
    bottom_drag,
    wet_mask,
    lon_green,
    lat_green,
):
    rows_here = elevation.shape[1]
    total_rows = rows_here * lat_size()
    wet_frac = wet_mask.astype(jnp.float32)
    source = wet_frac * elevation
    columns = source.shape[2]
    edge_rows = jnp.concatenate([lon_green[:HALO], lon_green[columns - HALO :]], axis=0)
    spare = 8 * ((2 * HALO + 7) // 8)
    gathers = []
    for stream in STREAMS:
        part = pick(source, 0, stream)
        mixed = jnp.einsum("krj,cj->krc", part, lon_green, precision=lax.Precision.HIGHEST)
        edges = jnp.einsum("ej,krj->ker", edge_rows, part, precision=lax.Precision.HIGHEST)
        edges = jnp.pad(edges, ((0, 0), (0, spare - 2 * HALO), (0, columns - rows_here)))
        packed = jnp.concatenate([mixed, edges], axis=1)
        gathers.append(lax.all_gather(packed, LAT, axis=1, tiled=True))

    fields = jnp.stack([ocean_depth, bottom_drag, wet_frac], axis=0)
    stack = jnp.concatenate([elevation - equilibrium, transport_u, transport_v, fields], axis=0)
    stack = widen_lat(widen_lon(stack, HALO, 2), HALO, 1)
    green_ext = widen_lat(lat_green, HALO, 0)
    gathers[0], stack, green_ext = lax.optimization_barrier((gathers[0], stack, green_ext))

    blocks = lat_size()
    block = rows_here + spare
    green_blocks = green_ext.reshape(green_ext.shape[0], blocks, rows_here)
    green_pad = jnp.pad(green_blocks, ((0, 0), (0, 0), (0, spare))).reshape(green_ext.shape[0], -1)
    size = lax.axis_size("lon")
    up = [(i, (i + 1) % size) for i in range(size)]
    down = [(j, i) for i, j in up]
    depth_ext, drag_ext, wet_ext = stack[36], stack[37], stack[38]
    first_row = lat_index() * rows_here - HALO
    stretch, coriolis = row_terms(first_row + jnp.arange(rows_here + 2 * HALO), total_rows)

    results = []
    for index, stream in enumerate(STREAMS):
        gathered = gathers[index]
        if results:
            gathered = lax.optimization_barrier((gathered, results[-1]))[0]
        freqs = tuple(FREQS[c] for c in stream)
        channels = 2 * len(stream)
        lanes = gathered.reshape(channels, blocks, block, columns)
        lanes = lanes[:, :, rows_here : rows_here + 2 * HALO, :rows_here]
        edge_sal = jnp.einsum("rbj,kbej->kre", green_blocks, lanes, precision=lax.Precision.HIGHEST)
        before = lax.ppermute(edge_sal[:, :, HALO:], "lon", up)
        after = lax.ppermute(edge_sal[:, :, :HALO], "lon", down)
        sal = jnp.einsum("rs,ksc->krc", green_pad, gathered, precision=lax.Precision.HIGHEST)
        sal = jnp.concatenate([before, sal, after], axis=2)
        potential = pick(stack, 0, stream) - sal
        flows = jnp.concatenate([pick(stack, 12, stream), pick(stack, 24, stream)], axis=0)

        east_slope, north_slope = slopes(potential, stretch[1:-1])
        flows = relax(
            flows,
            east_slope,
            north_slope,
            inner(depth_ext, 1),
            inner(drag_ext, 1),
            inner(wet_ext, 1),
            coriolis[1:-1],
            freqs,
        )
        flows = relax(
            flows,
            inner(east_slope, 1),
            inner(north_slope, 1),
            inner(depth_ext, 2),
            inner(drag_ext, 2),
            inner(wet_ext, 2),
            coriolis[2:-2],
            freqs,
        )
        east_ext = flows[:channels, 1:-1, :]
        north_ext = flows[channels:, :, 1:-1]
        elevation_next = surface(east_ext, north_ext, stretch[HALO:-HALO], wet_frac, freqs)
        flows = inner(flows, 1)
        results.append((elevation_next, flows[:channels], flows[channels:]))

    def merge(outputs):
        n = [len(stream) for stream in STREAMS]
        real = [out[:k] for out, k in zip(outputs, n)]
        imag = [out[k:] for out, k in zip(outputs, n)]
        return jnp.concatenate(real + imag, axis=0)

    return tuple(merge([result[i] for result in results]) for i in range(3))


def solution(mesh):
    lat_devices = mesh.shape["lat"]
    cores = 2 if lat_devices % 2 == 0 else 1
    devices = mesh.devices.reshape(mesh.shape["lon"], lat_devices // cores, cores)
    split = Mesh(devices, ("lon", "chip", "core"))
    grid = P(None, LAT, "lon")
    plane = P(LAT, "lon")
    placed = (grid, grid, grid, grid, plane, plane, plane, P("lon", None), plane)
    return jax.shard_map(
        per_device,
        mesh=split,
        in_specs=placed,
        out_specs=(grid, grid, grid),
        check_vma=False,
    )
```

```python
import math

import jax
import jax.numpy as jnp
from jax import lax
from jax.sharding import Mesh
from jax.sharding import PartitionSpec as P

FREQS = [1.9323, 2.0, 1.896, 2.0055, 1.0027, 0.9295]
VISCOSITY = 0.5
HALO = 3
LAT = ("chip", "core")


def lat_index():
    return lax.axis_index("chip") * lax.axis_size("core") + lax.axis_index("core")


def lat_size():
    return lax.axis_size("chip") * lax.axis_size("core")


def widen_lon(array, width, dim):
    size, length = lax.axis_size("lon"), array.shape[dim]
    up = [(i, (i + 1) % size) for i in range(size)]
    down = [(j, i) for i, j in up]
    last = lax.slice_in_dim(array, length - width, length, axis=dim)
    initial = lax.slice_in_dim(array, 0, width, axis=dim)
    before = lax.ppermute(last, "lon", up)
    after = lax.ppermute(initial, "lon", down)
    return jnp.concatenate([before, array, after], axis=dim)


def widen_lat(array, width, dim):
    size, length = lat_size(), array.shape[dim]
    up = [(i, i + 1) for i in range(size - 1)]
    down = [(j, i) for i, j in up]
    last = lax.slice_in_dim(array, length - width, length, axis=dim)
    initial = lax.slice_in_dim(array, 0, width, axis=dim)
    before = lax.ppermute(last, LAT, up)
    after = lax.ppermute(initial, LAT, down)
    return jnp.concatenate([before, array, after], axis=dim)


def row_terms(rows, nlat):
    angle = (-80.0 + 160.0 * (rows.astype(jnp.float32) + 0.5) / nlat) * (math.pi / 180.0)
    return ((1.0 / jnp.cos(angle))[:, None], (2.0 * jnp.sin(angle))[:, None])


def slopes(potential_ext, stretch):
    east_slope = (potential_ext[:, 1:-1, 2:] - potential_ext[:, 1:-1, :-2]) * 0.5 * stretch
    north_slope = (potential_ext[:, 2:, 1:-1] - potential_ext[:, :-2, 1:-1]) * 0.5
    return (east_slope, north_slope)


def cell_terms(drag_field, coriolis):
    damping = drag_field + 4.0 * VISCOSITY
    frequency = jnp.array(FREQS, jnp.float32)[:, None, None]
    det_real = damping * damping - frequency * frequency + coriolis * coriolis
    det_imag = 2.0 * damping * frequency
    magnitude = det_real * det_real + det_imag * det_imag
    return (damping, det_real, det_imag, magnitude)


def solve_cells(push_u, push_v, terms, wet_frac, coriolis):
    damping, det_real, det_imag, magnitude = terms
    frequency = jnp.array(FREQS, jnp.float32)[:, None, None]

    def combine(first, second, factor):
        top_real = damping * first[:6] - frequency * first[6:] + factor * coriolis * second[:6]
        top_imag = damping * first[6:] + frequency * first[:6] + factor * coriolis * second[6:]
        out_real = (top_real * det_real + top_imag * det_imag) / magnitude
        out_imag = (top_imag * det_real - top_real * det_imag) / magnitude
        return wet_frac * jnp.concatenate([out_real, out_imag], axis=0)

    return jnp.concatenate([combine(push_u, push_v, 1.0), combine(push_v, push_u, -1.0)], axis=0)


def inner(field, trim):
    return field[..., trim : field.shape[-2] - trim, trim : field.shape[-1] - trim]


def beside(flow_ext):
    return VISCOSITY * (
        flow_ext[:, :-2, 1:-1]
        + flow_ext[:, 2:, 1:-1]
        + flow_ext[:, 1:-1, :-2]
        + flow_ext[:, 1:-1, 2:]
    )


def relax(around, east_slope, north_slope, depth_field, terms, wet_frac, coriolis):
    push_u = -depth_field * east_slope + around[:12]
    push_v = -depth_field * north_slope + around[12:]
    return solve_cells(push_u, push_v, terms, wet_frac, coriolis)


def surface(east_ext, north_ext, stretch, wet_frac):
    spread = (east_ext[:, :, 2:] - east_ext[:, :, :-2]) * 0.5 * stretch + (
        north_ext[:, 2:, :] - north_ext[:, :-2, :]
    ) * 0.5
    frequency = jnp.array(FREQS, jnp.float32)[:, None, None]
    return wet_frac * jnp.concatenate([-spread[6:] / frequency, spread[:6] / frequency], axis=0)


def per_device(
    elevation,
    equilibrium,
    transport_u,
    transport_v,
    ocean_depth,
    bottom_drag,
    wet_mask,
    lon_green,
    lat_green,
):
    rows_here = elevation.shape[1]
    total_rows = rows_here * lat_size()
    wet_frac = wet_mask.astype(jnp.float32)
    source = wet_frac * elevation
    mixed = jnp.einsum("krj,cj->krc", source, lon_green, precision=lax.Precision.HIGHEST)
    columns = mixed.shape[2]
    edge_rows = jnp.concatenate([lon_green[:HALO], lon_green[columns - HALO :]], axis=0)
    edges = jnp.einsum("ej,krj->ker", edge_rows, source, precision=lax.Precision.HIGHEST)
    spare = 8 * ((2 * HALO + 7) // 8)
    edges = jnp.pad(edges, ((0, 0), (0, spare - 2 * HALO), (0, columns - rows_here)))
    packed = jnp.concatenate([mixed, edges], axis=1)
    gathered = lax.all_gather(packed, LAT, axis=1, tiled=True)

    fields = jnp.stack([ocean_depth, bottom_drag, wet_frac], axis=0)
    stack = jnp.concatenate([elevation - equilibrium, transport_u, transport_v, fields], axis=0)
    stack = widen_lat(widen_lon(stack, HALO, 2), HALO, 1)
    green_ext = widen_lat(lat_green, HALO, 0)
    depth_ext, drag_ext, wet_ext = stack[36], stack[37], stack[38]
    first_row = lat_index() * rows_here - HALO
    stretch, coriolis = row_terms(first_row + jnp.arange(rows_here + 2 * HALO), total_rows)
    around = beside(stack[12:36])
    terms_first = cell_terms(inner(drag_ext, 1), coriolis[1:-1])
    terms_second = cell_terms(inner(drag_ext, 2), coriolis[2:-2])
    blocks = lat_size()
    block = rows_here + spare
    green_blocks = green_ext.reshape(green_ext.shape[0], blocks, rows_here)
    green_pad = jnp.pad(green_blocks, ((0, 0), (0, 0), (0, spare))).reshape(green_ext.shape[0], -1)
    gathered, stack, green_pad, around, terms_first, terms_second = lax.optimization_barrier(
        (gathered, stack, green_pad, around, terms_first, terms_second)
    )
    lanes = gathered.reshape(12, blocks, block, columns)[:, :, rows_here : rows_here + 2 * HALO, :rows_here]
    edge_sal = jnp.einsum("rbj,kbej->kre", green_blocks, lanes, precision=lax.Precision.HIGHEST)
    size = lax.axis_size("lon")
    up = [(i, (i + 1) % size) for i in range(size)]
    down = [(j, i) for i, j in up]
    edge_sal, gathered = lax.optimization_barrier((edge_sal, gathered))
    before = lax.ppermute(edge_sal[:, :, HALO:], "lon", up)
    after = lax.ppermute(edge_sal[:, :, :HALO], "lon", down)
    sal = jnp.einsum("rs,ksc->krc", green_pad, gathered, precision=lax.Precision.HIGHEST)
    sal = jnp.concatenate([before, sal, after], axis=2)
    potential = stack[:12] - sal
    depth_ext, wet_ext = stack[36], stack[38]
    east_slope, north_slope = slopes(potential, stretch[1:-1])
    flows = relax(
        around,
        east_slope,
        north_slope,
        inner(depth_ext, 1),
        terms_first,
        inner(wet_ext, 1),
        coriolis[1:-1],
    )
    flows = relax(
        beside(flows),
        inner(east_slope, 1),
        inner(north_slope, 1),
        inner(depth_ext, 2),
        terms_second,
        inner(wet_ext, 2),
        coriolis[2:-2],
    )
    east_ext = flows[:12, 1:-1, :]
    north_ext = flows[12:, :, 1:-1]
    elevation_next = surface(east_ext, north_ext, stretch[HALO:-HALO], wet_frac)
    flows = inner(flows, 1)
    return (elevation_next, flows[:12], flows[12:])


def solution(mesh):
    lat_devices = mesh.shape["lat"]
    cores = 2 if lat_devices % 2 == 0 else 1
    devices = mesh.devices.reshape(mesh.shape["lon"], lat_devices // cores, cores)
    split = Mesh(devices, ("lon", "chip", "core"))
    grid = P(None, LAT, "lon")
    plane = P(LAT, "lon")
    placed = (grid, grid, grid, grid, plane, plane, plane, P("lon", None), plane)
    return jax.shard_map(
        per_device,
        mesh=split,
        in_specs=placed,
        out_specs=(grid, grid, grid),
        check_vma=False,
    )
```

```python
import math

import jax
import jax.numpy as jnp
from jax import lax
from jax.sharding import Mesh
from jax.sharding import PartitionSpec as P

FREQS = [1.9323, 2.0, 1.896, 2.0055, 1.0027, 0.9295]
VISCOSITY = 0.5
HALO = 3
LAT = ("half", "row", "core")
ROW = ("row", "core")


def lat_index():
    return (
        lax.axis_index("half") * lax.axis_size("row") + lax.axis_index("row")
    ) * lax.axis_size("core") + lax.axis_index("core")


def lat_size():
    return lax.axis_size("half") * lax.axis_size("row") * lax.axis_size("core")


def widen_lon(array, width, dim):
    size, length = lax.axis_size("lon"), array.shape[dim]
    up = [(i, (i + 1) % size) for i in range(size)]
    down = [(j, i) for i, j in up]
    last = lax.slice_in_dim(array, length - width, length, axis=dim)
    initial = lax.slice_in_dim(array, 0, width, axis=dim)
    before = lax.ppermute(last, "lon", up)
    after = lax.ppermute(initial, "lon", down)
    return jnp.concatenate([before, array, after], axis=dim)


def widen_lat(array, width, dim):
    size, length = lat_size(), array.shape[dim]
    up = [(i, i + 1) for i in range(size - 1)]
    down = [(j, i) for i, j in up]
    last = lax.slice_in_dim(array, length - width, length, axis=dim)
    initial = lax.slice_in_dim(array, 0, width, axis=dim)
    before = lax.ppermute(last, LAT, up)
    after = lax.ppermute(initial, LAT, down)
    return jnp.concatenate([before, array, after], axis=dim)


def row_terms(rows, nlat):
    angle = (-80.0 + 160.0 * (rows.astype(jnp.float32) + 0.5) / nlat) * (math.pi / 180.0)
    return ((1.0 / jnp.cos(angle))[:, None], (2.0 * jnp.sin(angle))[:, None])


def slopes(potential_ext, stretch):
    east_slope = (potential_ext[:, 1:-1, 2:] - potential_ext[:, 1:-1, :-2]) * 0.5 * stretch
    north_slope = (potential_ext[:, 2:, 1:-1] - potential_ext[:, :-2, 1:-1]) * 0.5
    return (east_slope, north_slope)


def solve_cells(push_u, push_v, drag_field, wet_frac, coriolis):
    damping = drag_field + 4.0 * VISCOSITY
    frequency = jnp.array(FREQS, jnp.float32)[:, None, None]
    det_real = damping * damping - frequency * frequency + coriolis * coriolis
    det_imag = 2.0 * damping * frequency
    magnitude = det_real * det_real + det_imag * det_imag

    def combine(first, second, factor):
        top_real = damping * first[:6] - frequency * first[6:] + factor * coriolis * second[:6]
        top_imag = damping * first[6:] + frequency * first[:6] + factor * coriolis * second[6:]
        out_real = (top_real * det_real + top_imag * det_imag) / magnitude
        out_imag = (top_imag * det_real - top_real * det_imag) / magnitude
        return wet_frac * jnp.concatenate([out_real, out_imag], axis=0)

    return jnp.concatenate([combine(push_u, push_v, 1.0), combine(push_v, push_u, -1.0)], axis=0)


def inner(field, trim):
    return field[..., trim : field.shape[-2] - trim, trim : field.shape[-1] - trim]


def relax(flow_ext, east_slope, north_slope, depth_field, drag_field, wet_frac, coriolis):
    beside_all = (
        flow_ext[:, :-2, 1:-1]
        + flow_ext[:, 2:, 1:-1]
        + flow_ext[:, 1:-1, :-2]
        + flow_ext[:, 1:-1, 2:]
    )
    push_u = -depth_field * east_slope + VISCOSITY * beside_all[:12]
    push_v = -depth_field * north_slope + VISCOSITY * beside_all[12:]
    return solve_cells(push_u, push_v, drag_field, wet_frac, coriolis)


def surface(east_ext, north_ext, stretch, wet_frac):
    spread = (east_ext[:, :, 2:] - east_ext[:, :, :-2]) * 0.5 * stretch + (
        north_ext[:, 2:, :] - north_ext[:, :-2, :]
    ) * 0.5
    frequency = jnp.array(FREQS, jnp.float32)[:, None, None]
    return wet_frac * jnp.concatenate([-spread[6:] / frequency, spread[:6] / frequency], axis=0)


def per_device(
    elevation,
    equilibrium,
    transport_u,
    transport_v,
    ocean_depth,
    bottom_drag,
    wet_mask,
    lon_green,
    lat_green,
):
    rows_here = elevation.shape[1]
    total_rows = rows_here * lat_size()
    wet_frac = wet_mask.astype(jnp.float32)
    source = wet_frac * elevation
    mixed = jnp.einsum("krj,cj->krc", source, lon_green, precision=lax.Precision.HIGHEST)
    gathered = lax.all_gather(mixed, ROW, axis=1, tiled=True)

    fields = jnp.stack([ocean_depth, bottom_drag, wet_frac], axis=0)
    stack = jnp.concatenate([elevation - equilibrium, transport_u, transport_v, fields], axis=0)
    stack = widen_lat(widen_lon(stack, HALO, 2), HALO, 1)
    green_ext = widen_lat(lat_green, HALO, 0)

    halves = lax.axis_size("half")
    half = lax.axis_index("half")
    green_split = green_ext.reshape(green_ext.shape[0], halves, -1)
    swap = [(i, (i + 1) % halves) for i in range(halves)]
    green_home = lax.dynamic_index_in_dim(green_split, half, axis=1, keepdims=False)
    lat_here, lat_count = lat_index(), lat_size()
    per_half = lat_count // halves
    own_split = lat_green.reshape(rows_here, halves, -1)

    def partner(i):
        return (i + per_half) % lat_count

    def columns_for(owner):
        return lax.dynamic_index_in_dim(own_split, (owner // per_half + 1) % halves, axis=1, keepdims=False)

    middle = lax.ppermute(columns_for(lat_here), LAT, [(i, partner(i)) for i in range(lat_count)])
    top = lax.ppermute(
        columns_for(lat_here + 1)[rows_here - HALO :],
        LAT,
        [(i, partner(i + 1)) for i in range(lat_count - 1)],
    )
    bottom = lax.ppermute(
        columns_for(lat_here - 1)[:HALO], LAT, [(i, partner(i - 1)) for i in range(1, lat_count)]
    )
    green_away = jnp.concatenate([top, middle, bottom], axis=0)
    for_partner = jnp.einsum("rs,ksc->krc", green_away, gathered, precision=lax.Precision.HIGHEST)
    back = [(j, i) for i, j in swap]
    from_partner = lax.ppermute(for_partner, "half", back)
    sal = jnp.einsum("rs,ksc->krc", green_home, gathered, precision=lax.Precision.HIGHEST)
    sal = sal + from_partner
    sal = widen_lon(sal, HALO, 2)
    potential = stack[:12] - sal
    flows = stack[12:36]
    depth_ext, drag_ext, wet_ext = stack[36], stack[37], stack[38]

    first_row = lat_index() * rows_here - HALO
    stretch, coriolis = row_terms(first_row + jnp.arange(rows_here + 2 * HALO), total_rows)
    east_slope, north_slope = slopes(potential, stretch[1:-1])
    flows = relax(
        flows,
        east_slope,
        north_slope,
        inner(depth_ext, 1),
        inner(drag_ext, 1),
        inner(wet_ext, 1),
        coriolis[1:-1],
    )
    flows = relax(
        flows,
        inner(east_slope, 1),
        inner(north_slope, 1),
        inner(depth_ext, 2),
        inner(drag_ext, 2),
        inner(wet_ext, 2),
        coriolis[2:-2],
    )
    east_ext = flows[:12, 1:-1, :]
    north_ext = flows[12:, :, 1:-1]
    elevation_next = surface(east_ext, north_ext, stretch[HALO:-HALO], wet_frac)
    flows = inner(flows, 1)
    return (elevation_next, flows[:12], flows[12:])


def solution(mesh):
    lat_devices = mesh.shape["lat"]
    devices = mesh.devices.reshape(mesh.shape["lon"], 2, lat_devices // 4, 2)
    split = Mesh(devices, ("lon", "half", "row", "core"))
    grid = P(None, LAT, "lon")
    plane = P(LAT, "lon")
    placed = (grid, grid, grid, grid, plane, plane, plane, P("lon", None), plane)
    return jax.shard_map(
        per_device,
        mesh=split,
        in_specs=placed,
        out_specs=(grid, grid, grid),
        check_vma=False,
    )
```

```python
import math

import jax
import jax.numpy as jnp
from jax import lax
from jax.sharding import Mesh
from jax.sharding import PartitionSpec as P

FREQS = [1.9323, 2.0, 1.896, 2.0055, 1.0027, 0.9295]
VISCOSITY = 0.5
HALO = 3
LAT = ("chip", "core")


def lat_index():
    return lax.axis_index("chip") * lax.axis_size("core") + lax.axis_index("core")


def lat_size():
    return lax.axis_size("chip") * lax.axis_size("core")


def widen_lon(array, width, dim):
    size, length = lax.axis_size("lon"), array.shape[dim]
    up = [(i, (i + 1) % size) for i in range(size)]
    down = [(j, i) for i, j in up]
    last = lax.slice_in_dim(array, length - width, length, axis=dim)
    initial = lax.slice_in_dim(array, 0, width, axis=dim)
    before = lax.ppermute(last, "lon", up)
    after = lax.ppermute(initial, "lon", down)
    return jnp.concatenate([before, array, after], axis=dim)


def widen_lat(array, width, dim):
    size, length = lat_size(), array.shape[dim]
    up = [(i, i + 1) for i in range(size - 1)]
    down = [(j, i) for i, j in up]
    last = lax.slice_in_dim(array, length - width, length, axis=dim)
    initial = lax.slice_in_dim(array, 0, width, axis=dim)
    before = lax.ppermute(last, LAT, up)
    after = lax.ppermute(initial, LAT, down)
    return jnp.concatenate([before, array, after], axis=dim)


def row_terms(rows, nlat):
    angle = (-80.0 + 160.0 * (rows.astype(jnp.float32) + 0.5) / nlat) * (math.pi / 180.0)
    return ((1.0 / jnp.cos(angle))[:, None], (2.0 * jnp.sin(angle))[:, None])


def slopes(potential_ext, stretch):
    east_slope = (potential_ext[:, 2:, 1:-1] - potential_ext[:, :-2, 1:-1]) * 0.5 * stretch
    north_slope = (potential_ext[:, 1:-1, 2:] - potential_ext[:, 1:-1, :-2]) * 0.5
    return (east_slope, north_slope)


def solve_cells(push_u, push_v, drag_field, wet_frac, coriolis):
    damping = drag_field + 4.0 * VISCOSITY
    frequency = jnp.array(FREQS, jnp.float32)[:, None, None]
    det_real = damping * damping - frequency * frequency + coriolis * coriolis
    det_imag = 2.0 * damping * frequency
    magnitude = det_real * det_real + det_imag * det_imag

    def combine(first, second, factor):
        top_real = damping * first[:6] - frequency * first[6:] + factor * coriolis * second[:6]
        top_imag = damping * first[6:] + frequency * first[:6] + factor * coriolis * second[6:]
        out_real = (top_real * det_real + top_imag * det_imag) / magnitude
        out_imag = (top_imag * det_real - top_real * det_imag) / magnitude
        return wet_frac * jnp.concatenate([out_real, out_imag], axis=0)

    return jnp.concatenate([combine(push_u, push_v, 1.0), combine(push_v, push_u, -1.0)], axis=0)


def inner(field, trim):
    return field[..., trim : field.shape[-2] - trim, trim : field.shape[-1] - trim]


def relax(flow_ext, east_slope, north_slope, depth_field, drag_field, wet_frac, coriolis):
    beside_all = (
        flow_ext[:, :-2, 1:-1]
        + flow_ext[:, 2:, 1:-1]
        + flow_ext[:, 1:-1, :-2]
        + flow_ext[:, 1:-1, 2:]
    )
    push_u = -depth_field * east_slope + VISCOSITY * beside_all[:12]
    push_v = -depth_field * north_slope + VISCOSITY * beside_all[12:]
    return solve_cells(push_u, push_v, drag_field, wet_frac, coriolis)


def surface(east_ext, north_ext, stretch, wet_frac):
    spread = (east_ext[:, 2:, :] - east_ext[:, :-2, :]) * 0.5 * stretch + (
        north_ext[:, :, 2:] - north_ext[:, :, :-2]
    ) * 0.5
    frequency = jnp.array(FREQS, jnp.float32)[:, None, None]
    return wet_frac * jnp.concatenate([-spread[6:] / frequency, spread[:6] / frequency], axis=0)


def per_device(
    elevation,
    equilibrium,
    transport_u,
    transport_v,
    ocean_depth,
    bottom_drag,
    wet_mask,
    lon_green,
    lat_green,
):
    rows_here = elevation.shape[1]
    total_rows = rows_here * lat_size()
    wet_frac = wet_mask.astype(jnp.float32)
    source = wet_frac * elevation
    mixed = jnp.einsum("krj,cj->krc", source, lon_green, precision=lax.Precision.HIGHEST)
    columns = mixed.shape[2]
    edge_rows = jnp.concatenate([lon_green[:HALO], lon_green[columns - HALO :]], axis=0)
    edges = jnp.einsum("ej,krj->ker", edge_rows, source, precision=lax.Precision.HIGHEST)
    spare = 8 * ((2 * HALO + 7) // 8)
    edges = jnp.pad(edges, ((0, 0), (0, spare - 2 * HALO), (0, columns - rows_here)))
    packed = jnp.concatenate([mixed, edges], axis=1)
    gathered = lax.all_gather(packed, LAT, axis=1, tiled=True)

    fields = jnp.stack([ocean_depth, bottom_drag, wet_frac], axis=0)
    stack = jnp.concatenate([elevation - equilibrium, transport_u, transport_v, fields], axis=0)
    stack = widen_lat(widen_lon(stack, HALO, 2), HALO, 1)
    green_ext = widen_lat(lat_green, HALO, 0)

    blocks = lat_size()
    block = rows_here + spare
    green_blocks = green_ext.reshape(green_ext.shape[0], blocks, rows_here)
    lanes = gathered.reshape(12, blocks, block, columns)[:, :, rows_here : rows_here + 2 * HALO, :rows_here]
    edge_sal = jnp.einsum("rbj,kbej->ker", green_blocks, lanes, precision=lax.Precision.HIGHEST)
    size = lax.axis_size("lon")
    up = [(i, (i + 1) % size) for i in range(size)]
    down = [(j, i) for i, j in up]
    before = lax.ppermute(edge_sal[:, HALO:], "lon", up)
    after = lax.ppermute(edge_sal[:, :HALO], "lon", down)
    green_pad = jnp.pad(green_blocks, ((0, 0), (0, 0), (0, spare))).reshape(green_ext.shape[0], -1)
    sal = jnp.einsum("rs,ksc->kcr", green_pad, gathered, precision=lax.Precision.HIGHEST)
    sal = jnp.concatenate([before, sal, after], axis=1)
    stack = jnp.swapaxes(stack, 1, 2)
    potential = stack[:12] - sal
    flows = stack[12:36]
    depth_ext, drag_ext, wet_ext = stack[36], stack[37], stack[38]

    first_row = lat_index() * rows_here - HALO
    stretch, coriolis = row_terms(first_row + jnp.arange(rows_here + 2 * HALO), total_rows)
    stretch, coriolis = stretch.T, coriolis.T
    east_slope, north_slope = slopes(potential, stretch[:, 1:-1])
    flows = relax(
        flows,
        east_slope,
        north_slope,
        inner(depth_ext, 1),
        inner(drag_ext, 1),
        inner(wet_ext, 1),
        coriolis[:, 1:-1],
    )
    flows = relax(
        flows,
        inner(east_slope, 1),
        inner(north_slope, 1),
        inner(depth_ext, 2),
        inner(drag_ext, 2),
        inner(wet_ext, 2),
        coriolis[:, 2:-2],
    )
    east_ext = flows[:12, :, 1:-1]
    north_ext = flows[12:, 1:-1, :]
    elevation_next = surface(east_ext, north_ext, stretch[:, HALO:-HALO], wet_frac.T)
    flows = jnp.swapaxes(inner(flows, 1), 1, 2)
    return (jnp.swapaxes(elevation_next, 1, 2), flows[:12], flows[12:])


def solution(mesh):
    lat_devices = mesh.shape["lat"]
    cores = 2 if lat_devices % 2 == 0 else 1
    devices = mesh.devices.reshape(mesh.shape["lon"], lat_devices // cores, cores)
    split = Mesh(devices, ("lon", "chip", "core"))
    grid = P(None, LAT, "lon")
    plane = P(LAT, "lon")
    placed = (grid, grid, grid, grid, plane, plane, plane, P("lon", None), plane)
    return jax.shard_map(
        per_device,
        mesh=split,
        in_specs=placed,
        out_specs=(grid, grid, grid),
        check_vma=False,
    )
```

```python
import math

import jax
import jax.numpy as jnp
from jax import lax
from jax.sharding import Mesh
from jax.sharding import PartitionSpec as P

FREQS = [1.9323, 2.0, 1.896, 2.0055, 1.0027, 0.9295]
VISCOSITY = 0.5
HALO = 3
LAT = ("chip", "core")


def lat_index():
    return lax.axis_index("chip") * lax.axis_size("core") + lax.axis_index("core")


def lat_size():
    return lax.axis_size("chip") * lax.axis_size("core")


def widen_lon(array, width, dim):
    size, length = lax.axis_size("lon"), array.shape[dim]
    up = [(i, (i + 1) % size) for i in range(size)]
    down = [(j, i) for i, j in up]
    last = lax.slice_in_dim(array, length - width, length, axis=dim)
    initial = lax.slice_in_dim(array, 0, width, axis=dim)
    before = lax.ppermute(last, "lon", up)
    after = lax.ppermute(initial, "lon", down)
    return jnp.concatenate([before, array, after], axis=dim)


def widen_lat(array, width, dim):
    size, length = lat_size(), array.shape[dim]
    up = [(i, i + 1) for i in range(size - 1)]
    down = [(j, i) for i, j in up]
    last = lax.slice_in_dim(array, length - width, length, axis=dim)
    initial = lax.slice_in_dim(array, 0, width, axis=dim)
    before = lax.ppermute(last, LAT, up)
    after = lax.ppermute(initial, LAT, down)
    return jnp.concatenate([before, array, after], axis=dim)


def row_terms(rows, nlat):
    angle = (-80.0 + 160.0 * (rows.astype(jnp.float32) + 0.5) / nlat) * (math.pi / 180.0)
    return ((1.0 / jnp.cos(angle))[:, None], (2.0 * jnp.sin(angle))[:, None])


def slopes(potential_ext, stretch):
    east_slope = (potential_ext[:, 1:-1, 2:] - potential_ext[:, 1:-1, :-2]) * 0.5 * stretch
    north_slope = (potential_ext[:, 2:, 1:-1] - potential_ext[:, :-2, 1:-1]) * 0.5
    return (east_slope, north_slope)


def solve_cells(push_u, push_v, drag_field, wet_frac, coriolis):
    damping = drag_field + 4.0 * VISCOSITY
    frequency = jnp.array(FREQS, jnp.float32)[:, None, None]
    det_real = damping * damping - frequency * frequency + coriolis * coriolis
    det_imag = 2.0 * damping * frequency
    magnitude = det_real * det_real + det_imag * det_imag

    def combine(first, second, factor):
        top_real = damping * first[:6] - frequency * first[6:] + factor * coriolis * second[:6]
        top_imag = damping * first[6:] + frequency * first[:6] + factor * coriolis * second[6:]
        out_real = (top_real * det_real + top_imag * det_imag) / magnitude
        out_imag = (top_imag * det_real - top_real * det_imag) / magnitude
        return wet_frac * jnp.concatenate([out_real, out_imag], axis=0)

    return jnp.concatenate([combine(push_u, push_v, 1.0), combine(push_v, push_u, -1.0)], axis=0)


def inner(field, trim):
    return field[..., trim : field.shape[-2] - trim, trim : field.shape[-1] - trim]


def relax(flow_ext, east_slope, north_slope, depth_field, drag_field, wet_frac, coriolis):
    beside_all = (
        flow_ext[:, :-2, 1:-1]
        + flow_ext[:, 2:, 1:-1]
        + flow_ext[:, 1:-1, :-2]
        + flow_ext[:, 1:-1, 2:]
    )
    push_u = -depth_field * east_slope + VISCOSITY * beside_all[:12]
    push_v = -depth_field * north_slope + VISCOSITY * beside_all[12:]
    return solve_cells(push_u, push_v, drag_field, wet_frac, coriolis)


def surface(east_ext, north_ext, stretch, wet_frac):
    spread = (east_ext[:, :, 2:] - east_ext[:, :, :-2]) * 0.5 * stretch + (
        north_ext[:, 2:, :] - north_ext[:, :-2, :]
    ) * 0.5
    frequency = jnp.array(FREQS, jnp.float32)[:, None, None]
    return wet_frac * jnp.concatenate([-spread[6:] / frequency, spread[:6] / frequency], axis=0)


def per_device(
    elevation,
    equilibrium,
    transport_u,
    transport_v,
    ocean_depth,
    bottom_drag,
    wet_mask,
    lon_green,
    lat_green,
):
    rows_here = elevation.shape[1]
    total_rows = rows_here * lat_size()
    wet_frac = wet_mask.astype(jnp.float32)
    source = wet_frac * elevation
    mixed = jnp.einsum("krj,cj->krc", source, lon_green, precision=lax.Precision.HIGHEST)
    columns = mixed.shape[2]
    edge_rows = jnp.concatenate([lon_green[:HALO], lon_green[columns - HALO :]], axis=0)
    edges = jnp.einsum("ej,krj->ker", edge_rows, source, precision=lax.Precision.HIGHEST)
    spare = 8 * ((2 * HALO + 7) // 8)
    edges = jnp.pad(edges, ((0, 0), (0, spare - 2 * HALO), (0, columns - rows_here)))
    packed = jnp.concatenate([mixed, edges], axis=1)
    gathered = lax.all_gather(packed, LAT, axis=1, tiled=True)

    fields = jnp.stack([ocean_depth, bottom_drag, wet_frac], axis=0)
    stack = jnp.concatenate([elevation - equilibrium, transport_u, transport_v, fields], axis=0)
    stack = widen_lat(widen_lon(stack, HALO, 2), HALO, 1)
    green_ext = widen_lat(lat_green, HALO, 0)

    blocks = lat_size()
    block = rows_here + spare
    green_blocks = green_ext.reshape(green_ext.shape[0], blocks, rows_here)
    lanes = gathered.reshape(12, blocks, block, columns)[:, :, rows_here:, :]
    green_lanes = jnp.pad(green_blocks, ((0, 0), (0, 0), (0, columns - rows_here)))
    edge_sal = jnp.einsum("rbj,kbej->kre", green_lanes, lanes, precision=lax.Precision.HIGHEST)
    size = lax.axis_size("lon")
    up = [(i, (i + 1) % size) for i in range(size)]
    down = [(j, i) for i, j in up]
    before = lax.ppermute(edge_sal[:, :, HALO : 2 * HALO], "lon", up)
    after = lax.ppermute(edge_sal[:, :, :HALO], "lon", down)
    green_pad = jnp.pad(green_blocks, ((0, 0), (0, 0), (0, spare))).reshape(green_ext.shape[0], -1)
    sal = jnp.einsum("rs,ksc->krc", green_pad, gathered, precision=lax.Precision.HIGHEST)
    sal = jnp.concatenate([before, sal, after], axis=2)
    potential = stack[:12] - sal
    flows = stack[12:36]
    depth_ext, drag_ext, wet_ext = stack[36], stack[37], stack[38]

    first_row = lat_index() * rows_here - HALO
    stretch, coriolis = row_terms(first_row + jnp.arange(rows_here + 2 * HALO), total_rows)
    east_slope, north_slope = slopes(potential, stretch[1:-1])
    flows = relax(
        flows,
        east_slope,
        north_slope,
        inner(depth_ext, 1),
        inner(drag_ext, 1),
        inner(wet_ext, 1),
        coriolis[1:-1],
    )
    flows = relax(
        flows,
        inner(east_slope, 1),
        inner(north_slope, 1),
        inner(depth_ext, 2),
        inner(drag_ext, 2),
        inner(wet_ext, 2),
        coriolis[2:-2],
    )
    east_ext = flows[:12, 1:-1, :]
    north_ext = flows[12:, :, 1:-1]
    elevation_next = surface(east_ext, north_ext, stretch[HALO:-HALO], wet_frac)
    flows = inner(flows, 1)
    return (elevation_next, flows[:12], flows[12:])


def solution(mesh):
    lat_devices = mesh.shape["lat"]
    cores = 2 if lat_devices % 2 == 0 else 1
    devices = mesh.devices.reshape(mesh.shape["lon"], lat_devices // cores, cores)
    split = Mesh(devices, ("lon", "chip", "core"))
    grid = P(None, LAT, "lon")
    plane = P(LAT, "lon")
    placed = (grid, grid, grid, grid, plane, plane, plane, P("lon", None), plane)
    return jax.shard_map(
        per_device,
        mesh=split,
        in_specs=placed,
        out_specs=(grid, grid, grid),
        check_vma=False,
    )
```
